128 devices in a mesh: dp: 8 (over z, x_lo), ctx: 16 (over y, x_hi, core).
Axes of the slice: x: 4 (x_hi: 2, x_lo: 2; x = x_hi * 2 + x_lo), y: 4, z: 4, core: 2. Of those that a mesh axis runs over, the one named last changes fastest.
Arguments:
- tokens: bfloat16 [8, 262144, 128], P('dp', 'ctx'), may hold values from -6 to 6
- cotangent: bfloat16 [8, 262144, 128], P('dp', 'ctx'), may hold values from -6 to 6
- w_gate_value: bfloat16 [128, 256], replicated, may hold values from -0.5 to 0.5
- w_first: bfloat16 [512, 512], replicated, may hold values from -0.25 to 0.25
- w_second: bfloat16 [512, 512], replicated, may hold values from -0.25 to 0.25
- w_up: bfloat16 [128, 256], replicated, may hold values from -0.5 to 0.5
- w_down: bfloat16 [256, 128], replicated, may hold values from -0.375 to 0.375
Outputs:
- output: bfloat16 [8, 262144, 128], P('dp', 'ctx')
- grad_tokens: bfloat16 [8, 262144, 128], P('dp', 'ctx')
- grad_gate_value: float32 [128, 256], replicated
- grad_first: float32 [512, 512], replicated
- grad_second: float32 [512, 512], replicated
- grad_up: float32 [128, 256], replicated
- grad_down: float32 [256, 128], replicated
The draws below stay inside these ranges and needn't reach their ends.
All inputs are finite; a program needn't handle non-finite values.
Results may differ from the reference program's by a relative error of at most 0.014.
Values may be sent and summed in bfloat16 or wider, within the bound.
No kernel may reach another device: no remote copies, remote signals or barrier semaphores. Data moves between devices by JAX's collectives and lax.ppermute only.
A program may use at most 256 MiB of HBM per device.

```python
import jax
import jax.numpy as jnp
from jax import lax

NB = 512
BS = 512
CH = 128
FF = 256
SEQLEN = 262144
SEQS = 8


def level_of(key, shape, cuts, low, top_value):
    factor_of, own = 1.0, jax.random.fold_in(key, 6)
    for axis_at, shards_of in cuts:
        steps = jnp.exp(jax.random.uniform(jax.random.fold_in(own, axis_at), (shards_of,), jnp.float32, low / len(cuts), top_value / len(cuts)))
        factor_of = factor_of * jnp.repeat(steps, shape[axis_at] // shards_of).reshape([-1 if axis == axis_at else 1 for axis in range(len(shape))])
    return factor_of


def centred(stream_key, extent, deviation, reach, pieces=(), dtype=jnp.bfloat16):
    drawn = jax.random.normal(stream_key, extent, jnp.float32) * deviation
    if len(pieces) > 0:
        drawn = level_of(stream_key, extent, pieces, -0.22, 0.18) * drawn
    return jnp.clip(drawn, min=-reach, max=reach).astype(dtype)


def setup_inputs(seed: int = 0) -> dict:
    splits = jax.random.split(jax.random.key(seed), 8)
    tokens = centred(splits[0], (SEQS, SEQLEN, CH), 1.0, 6.0, ((0, 8), (1, 16)))
    cotangent = centred(splits[1], (SEQS, SEQLEN, CH), 1.0, 6.0, ((0, 8), (1, 16)))
    w_gate_value = centred(splits[2], (CH, 2 * CH), CH ** -0.5, 0.5)
    w_first = centred(splits[3], (BS, BS), BS ** -0.5, 0.25)
    w_second = centred(splits[4], (NB, NB), NB ** -0.5, 0.25)
    w_up = centred(splits[5], (CH, FF), CH ** -0.5, 0.5)
    w_down = centred(splits[6], (FF, CH), FF ** -0.5, 0.375)
    return dict(tokens=tokens, cotangent=cotangent, w_gate_value=w_gate_value, w_first=w_first, w_second=w_second, w_up=w_up, w_down=w_down)


def silu_slope(pre):
    sigma = jax.nn.sigmoid(pre)
    return sigma * (1.0 + pre * (1.0 - sigma))


def one_sequence(seq_in, seq_cot, w_gate_value, w_first, w_second, w_up, w_down):
    f32 = jnp.float32
    bf16 = jnp.bfloat16
    projected = jnp.dot(seq_in, w_gate_value, preferred_element_type=f32)
    gate = jax.nn.sigmoid(projected[:, :CH])
    values = projected[:, CH:].astype(bf16)
    value_blocks = values.reshape(NB, BS, CH)
    first = jnp.einsum("ijc,jk->ikc", value_blocks.astype(f32), w_first.astype(f32)).astype(bf16)
    mixed = jnp.einsum("ikc,im->mkc", first.astype(f32), w_second.astype(f32)).astype(bf16).reshape(SEQLEN, CH)
    hidden = (seq_in.astype(f32) + gate * mixed.astype(f32)).astype(bf16)
    pre = jnp.dot(hidden, w_up, preferred_element_type=f32)
    activated = jax.nn.silu(pre).astype(bf16)
    output = (hidden.astype(f32) + jnp.dot(activated, w_down, preferred_element_type=f32)).astype(bf16)
    grad_down = jnp.dot(activated.T, seq_cot, preferred_element_type=f32)
    d_act = (jnp.dot(seq_cot, w_down.T, preferred_element_type=f32) * silu_slope(pre)).astype(bf16)
    grad_up = jnp.dot(hidden.T, d_act, preferred_element_type=f32)
    d_hidden = (seq_cot.astype(f32) + jnp.dot(d_act, w_up.T, preferred_element_type=f32)).astype(bf16)
    d_mixed = (d_hidden.astype(f32) * gate).astype(bf16).reshape(NB, BS, CH)
    d_gate = d_hidden.astype(f32) * mixed.astype(f32) * gate * (1.0 - gate)
    d_first = jnp.einsum("mkc,im->ikc", d_mixed.astype(f32), w_second.astype(f32)).astype(bf16)
    grad_second = jnp.einsum("ikc,mkc->im", first.astype(f32), d_mixed.astype(f32))
    d_values = jnp.einsum("ikc,jk->ijc", d_first.astype(f32), w_first.astype(f32)).reshape(SEQLEN, CH)
    grad_first = jnp.einsum("ijc,ikc->jk", value_blocks.astype(f32), d_first.astype(f32))
    d_projected = jnp.concatenate([d_gate, d_values], axis=1).astype(bf16)
    grad_gate_value = jnp.dot(seq_in.T, d_projected, preferred_element_type=f32)
    grad_tokens = (d_hidden.astype(f32) + jnp.dot(d_projected, w_gate_value.T, preferred_element_type=f32)).astype(bf16)
    return output, grad_tokens, (grad_gate_value, grad_first, grad_second, grad_up, grad_down)


def reference(tokens, cotangent, w_gate_value, w_first, w_second, w_up, w_down):
    f32 = jnp.float32
    start = (jnp.zeros((CH, 2 * CH), f32), jnp.zeros((BS, BS), f32), jnp.zeros((NB, NB), f32),
             jnp.zeros((CH, FF), f32), jnp.zeros((FF, CH), f32))

    def step_fn(totals, pair):
        output, grad_tokens, grads = one_sequence(pair[0], pair[1], w_gate_value, w_first, w_second, w_up, w_down)
        return jax.tree.map(lambda left, right: left + right, totals, grads), (output, grad_tokens)

    totals, outs = lax.scan(step_fn, start, (tokens, cotangent))
    scale = float(SEQS * SEQLEN) ** -0.5
    return (outs[0], outs[1], totals[0] * scale, totals[1] * scale, totals[2] * scale,
            totals[3] * scale, totals[4] * scale)
```

```python
import jax
import jax.numpy as jnp
from jax import lax
from jax.sharding import PartitionSpec as P

CHUNKS = 1


def silu_slope(pre):
    sigma = jax.nn.sigmoid(pre)
    return sigma * (1.0 + pre * (1.0 - sigma))


def a2a(x, axis):
    return lax.all_to_all(x, axis, 0, 0, tiled=True)


def all_reduce_a2a(flat):
    n_ctx = lax.axis_size("ctx")
    n_dp = lax.axis_size("dp")
    rows, width = flat.shape
    part = rows // n_ctx
    piece = part // n_dp
    a = a2a(flat.reshape(n_ctx, part, width), "ctx").sum(0)
    b = a2a(a.reshape(n_dp, piece, width), "dp").sum(0)
    c = a2a(jnp.broadcast_to(b[None], (n_dp, piece, width)), "dp").reshape(part, width)
    d = a2a(jnp.broadcast_to(c[None], (n_ctx, part, width)), "ctx").reshape(rows, width)
    return d


def body(tokens, cotangent, w_gate_value, w_first, w_second, w_up, w_down):
    f32 = jnp.float32
    bf16 = jnp.bfloat16
    n_ctx = lax.axis_size("ctx")
    n_dp = lax.axis_size("dp")
    seq_rows = tokens.shape[1]
    width = tokens.shape[2]
    block_size = w_first.shape[0]
    local_blocks = seq_rows // block_size
    all_blocks = w_second.shape[0]
    per_dev = block_size // n_ctx
    q_n = CHUNKS
    r_n = per_dev // q_n
    seq_in = tokens[0]
    seq_cot = cotangent[0]
    projected = jnp.dot(seq_in, w_gate_value, preferred_element_type=f32)
    gate = jax.nn.sigmoid(projected[:, :width])
    values = projected[:, width:].astype(bf16)
    value_blocks = values.reshape(local_blocks, block_size, width)
    wf = w_first.reshape(block_size, n_ctx, q_n, r_n)
    x5 = seq_in.reshape(local_blocks, n_ctx, q_n, r_n, width)
    c5 = seq_cot.reshape(local_blocks, n_ctx, q_n, r_n, width)
    g5 = gate.reshape(local_blocks, n_ctx, q_n, r_n, width)

    grad_down = jnp.zeros((w_down.shape[0], width), f32)
    grad_up = jnp.zeros((width, w_up.shape[1]), f32)
    grad_second = jnp.zeros((all_blocks, all_blocks), f32)
    d_values = jnp.zeros((local_blocks, block_size, width), f32)
    outs, d_hiddens, d_gates, gf_parts = [], [], [], []
    for q in range(q_n):
        wf_q = wf[:, :, q, :]
        first_q = jnp.einsum("ijc,jdr->dirc", value_blocks, wf_q, preferred_element_type=f32).astype(bf16)
        first_mid = a2a(first_q, "ctx").reshape(all_blocks, r_n, width)
        mixed_mid = jnp.einsum("ikc,im->mkc", first_mid, w_second, preferred_element_type=f32).astype(bf16)
        mixed = a2a(mixed_mid.reshape(n_ctx, local_blocks, r_n, width), "ctx")
        mixed = mixed.reshape(-1, width)
        xq = x5[:, :, q].transpose(1, 0, 2, 3).reshape(-1, width)
        cq = c5[:, :, q].transpose(1, 0, 2, 3).reshape(-1, width)
        gq = g5[:, :, q].transpose(1, 0, 2, 3).reshape(-1, width)
        mixed32 = mixed.astype(f32)
        hidden = (xq.astype(f32) + gq * mixed32).astype(bf16)
        pre = jnp.dot(hidden, w_up, preferred_element_type=f32)
        activated = jax.nn.silu(pre).astype(bf16)
        out_q = (hidden.astype(f32) + jnp.dot(activated, w_down, preferred_element_type=f32)).astype(bf16)
        grad_down = grad_down + jnp.dot(activated.T, cq, preferred_element_type=f32)
        d_act = (jnp.dot(cq, w_down.T, preferred_element_type=f32) * silu_slope(pre)).astype(bf16)
        grad_up = grad_up + jnp.dot(hidden.T, d_act, preferred_element_type=f32)
        d_hidden = (cq.astype(f32) + jnp.dot(d_act, w_up.T, preferred_element_type=f32)).astype(bf16)
        d_mixed = (d_hidden.astype(f32) * gq).astype(bf16)
        d_gate = d_hidden.astype(f32) * mixed32 * gq * (1.0 - gq)
        d_mixed_mid = a2a(d_mixed.reshape(n_ctx, local_blocks, r_n, width), "ctx")
        d_mixed_mid = d_mixed_mid.reshape(all_blocks, r_n, width)
        d_first_mid = jnp.einsum("mkc,im->ikc", d_mixed_mid, w_second, preferred_element_type=f32).astype(bf16)
        grad_second = grad_second + jnp.einsum(
            "ikc,mkc->im", first_mid, d_mixed_mid, preferred_element_type=f32
        )
        d_first = a2a(d_first_mid.reshape(n_ctx, local_blocks, r_n, width), "ctx")
        d_values = d_values + jnp.einsum("dirc,jdr->ijc", d_first, wf_q, preferred_element_type=f32)
        gf_parts.append(jnp.einsum("ijc,dirc->jdr", value_blocks, d_first, preferred_element_type=f32))
        outs.append(out_q.reshape(n_ctx, local_blocks, r_n, width))
        d_hiddens.append(d_hidden.reshape(n_ctx, local_blocks, r_n, width))
        d_gates.append(d_gate.reshape(n_ctx, local_blocks, r_n, width))

    def rows_of(parts):
        return jnp.stack(parts, axis=2).transpose(1, 0, 2, 3, 4).reshape(seq_rows, width)

    output = rows_of(outs)
    d_hidden = rows_of(d_hiddens)
    d_gate = rows_of(d_gates)
    grad_first = jnp.stack(gf_parts, axis=2).reshape(block_size, block_size)
    d_projected = jnp.concatenate([d_gate, d_values.reshape(seq_rows, width)], axis=1).astype(bf16)
    grad_gate_value = jnp.dot(seq_in.T, d_projected, preferred_element_type=f32)
    grad_tokens = (
        d_hidden.astype(f32) + jnp.dot(d_projected, w_gate_value.T, preferred_element_type=f32)
    ).astype(bf16)

    grads = (grad_gate_value, grad_first, grad_second, grad_up, grad_down)
    lane = 128
    flat = jnp.concatenate([g.reshape(-1, lane) for g in grads], axis=0)
    summed = all_reduce_a2a(flat)
    scale = float(seq_rows * n_ctx * n_dp) ** (-0.5)
    summed = summed * scale
    results = []
    at = 0
    for g in grads:
        n = g.size // lane
        results.append(summed[at:at + n].reshape(g.shape))
        at += n
    return (output[None], grad_tokens[None], *results)


def solution(mesh):
    placed = (P("dp", "ctx", None), P("dp", "ctx", None), P(), P(), P(), P(), P())
    return jax.shard_map(
        body,
        mesh=mesh,
        in_specs=placed,
        out_specs=(P("dp", "ctx", None), P("dp", "ctx", None), P(), P(), P(), P(), P()),
        check_vma=False,
    )
```

```python
import jax
import jax.numpy as jnp
from jax import lax
from jax.sharding import PartitionSpec as P

CHUNKS = 2


def silu_slope(pre):
    sigma = jax.nn.sigmoid(pre)
    return sigma * (1.0 + pre * (1.0 - sigma))


def a2a(x, axis):
    return lax.all_to_all(x, axis, 0, 0, tiled=True)


def all_reduce_a2a(flat):
    n_ctx = lax.axis_size("ctx")
    n_dp = lax.axis_size("dp")
    rows, width = flat.shape
    part = rows // n_ctx
    piece = part // n_dp
    a = a2a(flat.reshape(n_ctx, part, width), "ctx").sum(0)
    b = a2a(a.reshape(n_dp, piece, width), "dp").sum(0)
    c = a2a(jnp.broadcast_to(b[None], (n_dp, piece, width)), "dp").reshape(part, width)
    d = a2a(jnp.broadcast_to(c[None], (n_ctx, part, width)), "ctx").reshape(rows, width)
    return d


def body(tokens, cotangent, w_gate_value, w_first, w_second, w_up, w_down):
    f32 = jnp.float32
    bf16 = jnp.bfloat16
    n_ctx = lax.axis_size("ctx")
    n_dp = lax.axis_size("dp")
    seq_rows = tokens.shape[1]
    width = tokens.shape[2]
    block_size = w_first.shape[0]
    local_blocks = seq_rows // block_size
    all_blocks = w_second.shape[0]
    per_dev = block_size // n_ctx
    q_n = CHUNKS
    r_n = per_dev // q_n
    seq_in = tokens[0]
    seq_cot = cotangent[0]
    projected = jnp.dot(seq_in, w_gate_value, preferred_element_type=f32)
    gate = jax.nn.sigmoid(projected[:, :width])
    values = projected[:, width:].astype(bf16)
    value_blocks = values.reshape(local_blocks, block_size, width)
    wf = w_first.reshape(block_size, n_ctx, q_n, r_n)
    x5 = seq_in.reshape(local_blocks, n_ctx, q_n, r_n, width)
    c5 = seq_cot.reshape(local_blocks, n_ctx, q_n, r_n, width)
    g5 = gate.reshape(local_blocks, n_ctx, q_n, r_n, width)

    grad_down = jnp.zeros((w_down.shape[0], width), f32)
    grad_up = jnp.zeros((width, w_up.shape[1]), f32)
    grad_second = jnp.zeros((all_blocks, all_blocks), f32)
    d_values = jnp.zeros((local_blocks, block_size, width), f32)
    outs, d_hiddens, d_gates, gf_parts = [], [], [], []
    for q in range(q_n):
        wf_q = wf[:, :, q, :]
        first_q = jnp.einsum("ijc,jdr->dirc", value_blocks, wf_q, preferred_element_type=f32).astype(bf16)
        first_mid = a2a(first_q, "ctx").reshape(all_blocks, r_n, width)
        mixed_mid = jnp.einsum("ikc,im->mkc", first_mid, w_second, preferred_element_type=f32).astype(bf16)
        mixed = a2a(mixed_mid.reshape(n_ctx, local_blocks, r_n, width), "ctx")
        mixed = mixed.reshape(-1, width)
        xq = x5[:, :, q].transpose(1, 0, 2, 3).reshape(-1, width)
        cq = c5[:, :, q].transpose(1, 0, 2, 3).reshape(-1, width)
        gq = g5[:, :, q].transpose(1, 0, 2, 3).reshape(-1, width)
        mixed32 = mixed.astype(f32)
        hidden = (xq.astype(f32) + gq * mixed32).astype(bf16)
        pre = jnp.dot(hidden, w_up, preferred_element_type=f32)
        activated = jax.nn.silu(pre).astype(bf16)
        out_q = (hidden.astype(f32) + jnp.dot(activated, w_down, preferred_element_type=f32)).astype(bf16)
        grad_down = grad_down + jnp.dot(activated.T, cq, preferred_element_type=f32)
        d_act = (jnp.dot(cq, w_down.T, preferred_element_type=f32) * silu_slope(pre)).astype(bf16)
        grad_up = grad_up + jnp.dot(hidden.T, d_act, preferred_element_type=f32)
        d_hidden = (cq.astype(f32) + jnp.dot(d_act, w_up.T, preferred_element_type=f32)).astype(bf16)
        d_mixed = (d_hidden.astype(f32) * gq).astype(bf16)
        d_gate = d_hidden.astype(f32) * mixed32 * gq * (1.0 - gq)
        d_mixed_mid = a2a(d_mixed.reshape(n_ctx, local_blocks, r_n, width), "ctx")
        d_mixed_mid = d_mixed_mid.reshape(all_blocks, r_n, width)
        d_first_mid = jnp.einsum("mkc,im->ikc", d_mixed_mid, w_second, preferred_element_type=f32).astype(bf16)
        grad_second = grad_second + jnp.einsum(
            "ikc,mkc->im", first_mid, d_mixed_mid, preferred_element_type=f32
        )
        d_first = a2a(d_first_mid.reshape(n_ctx, local_blocks, r_n, width), "ctx")
        d_values = d_values + jnp.einsum("dirc,jdr->ijc", d_first, wf_q, preferred_element_type=f32)
        gf_parts.append(jnp.einsum("ijc,dirc->jdr", value_blocks, d_first, preferred_element_type=f32))
        outs.append(out_q.reshape(n_ctx, local_blocks, r_n, width))
        d_hiddens.append(d_hidden.reshape(n_ctx, local_blocks, r_n, width))
        d_gates.append(d_gate.reshape(n_ctx, local_blocks, r_n, width))

    def rows_of(parts):
        return jnp.stack(parts, axis=2).transpose(1, 0, 2, 3, 4).reshape(seq_rows, width)

    output = rows_of(outs)
    d_hidden = rows_of(d_hiddens)
    d_gate = rows_of(d_gates)
    grad_first = jnp.stack(gf_parts, axis=2).reshape(block_size, block_size)
    d_projected = jnp.concatenate([d_gate, d_values.reshape(seq_rows, width)], axis=1).astype(bf16)
    grad_gate_value = jnp.dot(seq_in.T, d_projected, preferred_element_type=f32)
    grad_tokens = (
        d_hidden.astype(f32) + jnp.dot(d_projected, w_gate_value.T, preferred_element_type=f32)
    ).astype(bf16)

    grads = (grad_gate_value, grad_first, grad_second, grad_up, grad_down)
    lane = 128
    flat = jnp.concatenate([g.reshape(-1, lane) for g in grads], axis=0)
    summed = all_reduce_a2a(flat)
    scale = float(seq_rows * n_ctx * n_dp) ** (-0.5)
    summed = summed * scale
    results = []
    at = 0
    for g in grads:
        n = g.size // lane
        results.append(summed[at:at + n].reshape(g.shape))
        at += n
    return (output[None], grad_tokens[None], *results)


def solution(mesh):
    placed = (P("dp", "ctx", None), P("dp", "ctx", None), P(), P(), P(), P(), P())
    return jax.shard_map(
        body,
        mesh=mesh,
        in_specs=placed,
        out_specs=(P("dp", "ctx", None), P("dp", "ctx", None), P(), P(), P(), P(), P()),
        check_vma=False,
    )
```

```python
import jax
import jax.numpy as jnp
from jax import lax
from jax.sharding import PartitionSpec as P

CHUNKS = 1


def silu_slope(pre):
    sigma = jax.nn.sigmoid(pre)
    return sigma * (1.0 + pre * (1.0 - sigma))


def a2a(x, axis):
    return lax.all_to_all(x, axis, 0, 0, tiled=True)


def all_reduce_a2a(flat):
    n_ctx = lax.axis_size("ctx")
    n_dp = lax.axis_size("dp")
    rows, width = flat.shape
    part = rows // n_ctx
    piece = part // n_dp
    a = a2a(flat.reshape(n_ctx, part, width), "ctx").sum(0)
    b = a2a(a.reshape(n_dp, piece, width), "dp").sum(0)
    c = a2a(jnp.broadcast_to(b[None], (n_dp, piece, width)), "dp").reshape(part, width)
    d = a2a(jnp.broadcast_to(c[None], (n_ctx, part, width)), "ctx").reshape(rows, width)
    return d


def body(tokens, cotangent, w_gate_value, w_first, w_second, w_up, w_down):
    f32 = jnp.float32
    bf16 = jnp.bfloat16
    n_ctx = lax.axis_size("ctx")
    n_dp = lax.axis_size("dp")
    seq_rows = tokens.shape[1]
    width = tokens.shape[2]
    block_size = w_first.shape[0]
    local_blocks = seq_rows // block_size
    all_blocks = w_second.shape[0]
    per_dev = block_size // n_ctx
    q_n = CHUNKS
    r_n = per_dev // q_n
    seq_in = tokens[0]
    seq_cot = cotangent[0]
    projected = jnp.dot(seq_in, w_gate_value, preferred_element_type=f32)
    gate = jax.nn.sigmoid(projected[:, :width])
    values = projected[:, width:].astype(bf16)
    value_blocks = values.reshape(local_blocks, block_size, width)
    wf = w_first.reshape(block_size, n_ctx, q_n, r_n)
    x5 = seq_in.reshape(local_blocks, n_ctx, q_n, r_n, width)
    c5 = seq_cot.reshape(local_blocks, n_ctx, q_n, r_n, width)
    g5 = gate.reshape(local_blocks, n_ctx, q_n, r_n, width)

    grad_down = jnp.zeros((w_down.shape[0], width), f32)
    grad_up = jnp.zeros((width, w_up.shape[1]), f32)
    grad_second = jnp.zeros((all_blocks, all_blocks), f32)
    d_values = jnp.zeros((local_blocks, block_size, width), f32)
    outs, d_hiddens, d_gates, gf_parts = [], [], [], []
    for q in range(q_n):
        wf_q = wf[:, :, q, :]
        first_q = jnp.einsum("ijc,jdr->dirc", value_blocks, wf_q, preferred_element_type=f32).astype(bf16)
        first_mid = a2a(first_q, "ctx").reshape(all_blocks, r_n, width)
        mixed_mid = jnp.einsum("ikc,im->mkc", first_mid, w_second, preferred_element_type=f32).astype(bf16)
        mixed = a2a(mixed_mid.reshape(n_ctx, local_blocks, r_n, width), "ctx")
        mixed = mixed.reshape(-1, width)
        xq = x5[:, :, q].transpose(1, 0, 2, 3).reshape(-1, width)
        cq = c5[:, :, q].transpose(1, 0, 2, 3).reshape(-1, width)
        gq = g5[:, :, q].transpose(1, 0, 2, 3).reshape(-1, width)
        mixed32 = mixed.astype(f32)
        hidden = (xq.astype(f32) + gq * mixed32).astype(bf16)
        pre = jnp.dot(hidden, w_up, preferred_element_type=f32)
        activated = jax.nn.silu(pre).astype(bf16)
        out_q = (hidden.astype(f32) + jnp.dot(activated, w_down, preferred_element_type=f32)).astype(bf16)
        grad_down = grad_down + jnp.dot(activated.T, cq, preferred_element_type=f32)
        d_act = (jnp.dot(cq, w_down.T, preferred_element_type=f32) * silu_slope(pre)).astype(bf16)
        grad_up = grad_up + jnp.dot(hidden.T, d_act, preferred_element_type=f32)
        d_hidden = (cq.astype(f32) + jnp.dot(d_act, w_up.T, preferred_element_type=f32)).astype(bf16)
        d_mixed = (d_hidden.astype(f32) * gq).astype(bf16)
        d_gate = d_hidden.astype(f32) * mixed32 * gq * (1.0 - gq)
        d_mixed_mid = a2a(d_mixed.reshape(n_ctx, local_blocks, r_n, width), "ctx")
        d_mixed_mid = d_mixed_mid.reshape(all_blocks, r_n, width)
        d_first_mid = jnp.einsum("mkc,im->ikc", d_mixed_mid, w_second, preferred_element_type=f32).astype(bf16)
        grad_second = grad_second + jnp.einsum(
            "ikc,mkc->im", first_mid, d_mixed_mid, preferred_element_type=f32
        )
        d_first = a2a(d_first_mid.reshape(n_ctx, local_blocks, r_n, width), "ctx")
        d_values = d_values + jnp.einsum("dirc,jdr->ijc", d_first, wf_q, preferred_element_type=f32)
        gf_parts.append(jnp.einsum("ijc,dirc->jdr", value_blocks, d_first, preferred_element_type=f32))
        outs.append(out_q.reshape(n_ctx, local_blocks, r_n, width))
        d_hiddens.append(d_hidden.reshape(n_ctx, local_blocks, r_n, width))
        d_gates.append(d_gate.reshape(n_ctx, local_blocks, r_n, width))

    def rows_of(parts):
        return jnp.stack(parts, axis=2).transpose(1, 0, 2, 3, 4).reshape(seq_rows, width)

    output = rows_of(outs)
    d_hidden = rows_of(d_hiddens)
    d_gate = rows_of(d_gates)
    grad_first = jnp.stack(gf_parts, axis=2).reshape(block_size, block_size)
    d_projected = jnp.concatenate([d_gate, d_values.reshape(seq_rows, width)], axis=1).astype(bf16)
    grad_gate_value = jnp.dot(seq_in.T, d_projected, preferred_element_type=f32)
    grad_tokens = (
        d_hidden.astype(f32) + jnp.dot(d_projected, w_gate_value.T, preferred_element_type=f32)
    ).astype(bf16)

    early = lax.psum((grad_second, grad_up, grad_down), ("dp", "ctx"))
    late = (grad_gate_value, grad_first)
    lane = 128
    flat = jnp.concatenate([g.reshape(-1, lane) for g in late], axis=0)
    summed = all_reduce_a2a(flat)
    scale = float(seq_rows * n_ctx * n_dp) ** (-0.5)
    summed = summed * scale
    late_out = []
    at = 0
    for g in late:
        n = g.size // lane
        late_out.append(summed[at:at + n].reshape(g.shape))
        at += n
    results = [late_out[0], late_out[1], early[0] * scale, early[1] * scale, early[2] * scale]
    return (output[None], grad_tokens[None], *results)


def solution(mesh):
    placed = (P("dp", "ctx", None), P("dp", "ctx", None), P(), P(), P(), P(), P())
    return jax.shard_map(
        body,
        mesh=mesh,
        in_specs=placed,
        out_specs=(P("dp", "ctx", None), P("dp", "ctx", None), P(), P(), P(), P(), P()),
        check_vma=False,
    )
```

```python
import jax
import jax.numpy as jnp
from jax import lax
from jax.sharding import PartitionSpec as P

CHUNKS = 1


def silu_slope(pre):
    sigma = jax.nn.sigmoid(pre)
    return sigma * (1.0 + pre * (1.0 - sigma))


def a2a(x, axis):
    return lax.all_to_all(x, axis, 0, 0, tiled=True)


def all_reduce_a2a(flat):
    n_ctx = lax.axis_size("ctx")
    n_dp = lax.axis_size("dp")
    rows, width = flat.shape
    part = rows // n_ctx
    piece = part // n_dp
    a = a2a(flat.reshape(n_ctx, part, width), "ctx").sum(0)
    b = a2a(a.reshape(n_dp, piece, width), "dp").sum(0)
    c = a2a(jnp.broadcast_to(b[None], (n_dp, piece, width)), "dp").reshape(part, width)
    d = a2a(jnp.broadcast_to(c[None], (n_ctx, part, width)), "ctx").reshape(rows, width)
    return d


def body(tokens, cotangent, w_gate_value, w_first, w_second, w_up, w_down):
    f32 = jnp.float32
    bf16 = jnp.bfloat16
    n_ctx = lax.axis_size("ctx")
    n_dp = lax.axis_size("dp")
    seq_rows = tokens.shape[1]
    width = tokens.shape[2]
    block_size = w_first.shape[0]
    local_blocks = seq_rows // block_size
    all_blocks = w_second.shape[0]
    per_dev = block_size // n_ctx
    q_n = CHUNKS
    r_n = per_dev // q_n
    seq_in = tokens[0]
    seq_cot = cotangent[0]
    projected = jnp.dot(seq_in, w_gate_value, preferred_element_type=f32)
    gate = jax.nn.sigmoid(projected[:, :width])
    values = projected[:, width:].astype(bf16)
    value_blocks = values.reshape(local_blocks, block_size, width)
    wf = w_first.reshape(block_size, n_ctx, q_n, r_n)
    x5 = seq_in.reshape(local_blocks, n_ctx, q_n, r_n, width)
    c5 = seq_cot.reshape(local_blocks, n_ctx, q_n, r_n, width)
    g5 = gate.reshape(local_blocks, n_ctx, q_n, r_n, width)

    grad_down = jnp.zeros((w_down.shape[0], width), f32)
    grad_up = jnp.zeros((width, w_up.shape[1]), f32)
    grad_second = jnp.zeros((all_blocks, all_blocks), f32)
    d_values = jnp.zeros((local_blocks, block_size, width), f32)
    outs, d_hiddens, d_gates, gf_parts = [], [], [], []
    for q in range(q_n):
        wf_q = wf[:, :, q, :]
        first_q = jnp.einsum("ijc,jdr->dirc", value_blocks, wf_q, preferred_element_type=f32).astype(bf16)
        first_mid = a2a(first_q, "ctx").reshape(all_blocks, r_n, width)
        mixed_mid = jnp.einsum("im,ikc->mkc", w_second, first_mid, preferred_element_type=f32).astype(bf16)
        mixed = a2a(mixed_mid.reshape(n_ctx, local_blocks, r_n, width), "ctx")
        mixed = mixed.transpose(1, 0, 2, 3).reshape(-1, width)
        xq = x5[:, :, q].reshape(-1, width)
        cq = c5[:, :, q].reshape(-1, width)
        gq = g5[:, :, q].reshape(-1, width)
        mixed32 = mixed.astype(f32)
        hidden = (xq.astype(f32) + gq * mixed32).astype(bf16)
        pre = jnp.dot(hidden, w_up, preferred_element_type=f32)
        activated = jax.nn.silu(pre).astype(bf16)
        out_q = (hidden.astype(f32) + jnp.dot(activated, w_down, preferred_element_type=f32)).astype(bf16)
        grad_down = grad_down + jnp.dot(activated.T, cq, preferred_element_type=f32)
        d_act = (jnp.dot(cq, w_down.T, preferred_element_type=f32) * silu_slope(pre)).astype(bf16)
        grad_up = grad_up + jnp.dot(hidden.T, d_act, preferred_element_type=f32)
        d_hidden = (cq.astype(f32) + jnp.dot(d_act, w_up.T, preferred_element_type=f32)).astype(bf16)
        d_mixed = (d_hidden.astype(f32) * gq).astype(bf16)
        d_gate = d_hidden.astype(f32) * mixed32 * gq * (1.0 - gq)
        d_mixed_mid = a2a(d_mixed.reshape(local_blocks, n_ctx, r_n, width).transpose(1, 0, 2, 3), "ctx")
        d_mixed_mid = d_mixed_mid.reshape(all_blocks, r_n, width)
        d_first_mid = jnp.einsum("im,mkc->ikc", w_second, d_mixed_mid, preferred_element_type=f32).astype(bf16)
        grad_second = grad_second + jnp.einsum(
            "ikc,mkc->im", first_mid, d_mixed_mid, preferred_element_type=f32
        )
        d_first = a2a(d_first_mid.reshape(n_ctx, local_blocks, r_n, width), "ctx")
        d_values = d_values + jnp.einsum("dirc,jdr->ijc", d_first, wf_q, preferred_element_type=f32)
        gf_parts.append(jnp.einsum("ijc,dirc->jdr", value_blocks, d_first, preferred_element_type=f32))
        outs.append(out_q.reshape(local_blocks, n_ctx, r_n, width))
        d_hiddens.append(d_hidden.reshape(local_blocks, n_ctx, r_n, width))
        d_gates.append(d_gate.reshape(local_blocks, n_ctx, r_n, width))

    def rows_of(parts):
        if len(parts) == 1:
            return parts[0].reshape(seq_rows, width)
        return jnp.stack(parts, axis=2).reshape(seq_rows, width)

    output = rows_of(outs)
    d_hidden = rows_of(d_hiddens)
    d_gate = rows_of(d_gates)
    grad_first = jnp.stack(gf_parts, axis=2).reshape(block_size, block_size)
    d_projected = jnp.concatenate([d_gate, d_values.reshape(seq_rows, width)], axis=1).astype(bf16)
    grad_gate_value = jnp.dot(seq_in.T, d_projected, preferred_element_type=f32)
    grad_tokens = (
        d_hidden.astype(f32) + jnp.dot(d_projected, w_gate_value.T, preferred_element_type=f32)
    ).astype(bf16)

    grads = (grad_gate_value, grad_first, grad_second, grad_up, grad_down)
    lane = 128
    flat = jnp.concatenate([g.reshape(-1, lane) for g in grads], axis=0)
    summed = all_reduce_a2a(flat)
    scale = float(seq_rows * n_ctx * n_dp) ** (-0.5)
    summed = summed * scale
    results = []
    at = 0
    for g in grads:
        n = g.size // lane
        results.append(summed[at:at + n].reshape(g.shape))
        at += n
    return (output[None], grad_tokens[None], *results)


def solution(mesh):
    placed = (P("dp", "ctx", None), P("dp", "ctx", None), P(), P(), P(), P(), P())
    return jax.shard_map(
        body,
        mesh=mesh,
        in_specs=placed,
        out_specs=(P("dp", "ctx", None), P("dp", "ctx", None), P(), P(), P(), P(), P()),
        check_vma=False,
    )
```

```python
import jax
import jax.numpy as jnp
from jax import lax
from jax.sharding import PartitionSpec as P

CHUNKS = 1


def silu_slope(pre):
    sigma = jax.nn.sigmoid(pre)
    return sigma * (1.0 + pre * (1.0 - sigma))


def a2a(x, axis, groups=None):
    return lax.all_to_all(x, axis, 0, 0, tiled=True, axis_index_groups=groups)


def all_reduce_a2a(flat):
    n_ctx = lax.axis_size("ctx")
    n_dp = lax.axis_size("dp")
    rows, width = flat.shape
    core = lax.axis_index("ctx") % 2
    pairs = [(i, i ^ 1) for i in range(n_ctx)]
    groups = [list(range(0, n_ctx, 2)), list(range(1, n_ctx, 2))]
    chips = n_ctx // 2
    half = rows // 2
    part = half // chips
    piece = part // n_dp
    halves = flat.reshape(2, half, width)
    mine = jnp.where(core == 0, halves[0], halves[1])
    other = jnp.where(core == 0, halves[1], halves[0])
    s1 = mine + lax.ppermute(other, "ctx", pairs)
    a = a2a(s1.reshape(chips, part, width), "ctx", groups).sum(0)
    b = a2a(a.reshape(n_dp, piece, width), "dp").sum(0)
    c = a2a(jnp.broadcast_to(b[None], (n_dp, piece, width)), "dp").reshape(part, width)
    d = a2a(jnp.broadcast_to(c[None], (chips, part, width)), "ctx", groups).reshape(half, width)
    e = lax.ppermute(d, "ctx", pairs)
    return jnp.where(core == 0, jnp.concatenate([d, e]), jnp.concatenate([e, d]))


def body(tokens, cotangent, w_gate_value, w_first, w_second, w_up, w_down):
    f32 = jnp.float32
    bf16 = jnp.bfloat16
    n_ctx = lax.axis_size("ctx")
    n_dp = lax.axis_size("dp")
    seq_rows = tokens.shape[1]
    width = tokens.shape[2]
    block_size = w_first.shape[0]
    local_blocks = seq_rows // block_size
    all_blocks = w_second.shape[0]
    per_dev = block_size // n_ctx
    q_n = CHUNKS
    r_n = per_dev // q_n
    seq_in = tokens[0]
    seq_cot = cotangent[0]
    projected = jnp.dot(seq_in, w_gate_value, preferred_element_type=f32)
    gate = jax.nn.sigmoid(projected[:, :width])
    values = projected[:, width:].astype(bf16)
    value_blocks = values.reshape(local_blocks, block_size, width)
    wf = w_first.reshape(block_size, n_ctx, q_n, r_n)
    x5 = seq_in.reshape(local_blocks, n_ctx, q_n, r_n, width)
    c5 = seq_cot.reshape(local_blocks, n_ctx, q_n, r_n, width)
    g5 = gate.reshape(local_blocks, n_ctx, q_n, r_n, width)

    grad_down = jnp.zeros((w_down.shape[0], width), f32)
    grad_up = jnp.zeros((width, w_up.shape[1]), f32)
    grad_second = jnp.zeros((all_blocks, all_blocks), f32)
    d_values = jnp.zeros((local_blocks, block_size, width), f32)
    outs, d_hiddens, d_gates, gf_parts = [], [], [], []
    for q in range(q_n):
        wf_q = wf[:, :, q, :]
        first_q = jnp.einsum("ijc,jdr->dirc", value_blocks, wf_q, preferred_element_type=f32).astype(bf16)
        first_mid = a2a(first_q, "ctx").reshape(all_blocks, r_n, width)
        mixed_mid = jnp.einsum("ikc,im->mkc", first_mid, w_second, preferred_element_type=f32).astype(bf16)
        mixed = a2a(mixed_mid.reshape(n_ctx, local_blocks, r_n, width), "ctx")
        mixed = mixed.reshape(-1, width)
        xq = x5[:, :, q].transpose(1, 0, 2, 3).reshape(-1, width)
        cq = c5[:, :, q].transpose(1, 0, 2, 3).reshape(-1, width)
        gq = g5[:, :, q].transpose(1, 0, 2, 3).reshape(-1, width)
        mixed32 = mixed.astype(f32)
        hidden = (xq.astype(f32) + gq * mixed32).astype(bf16)
        pre = jnp.dot(hidden, w_up, preferred_element_type=f32)
        activated = jax.nn.silu(pre).astype(bf16)
        out_q = (hidden.astype(f32) + jnp.dot(activated, w_down, preferred_element_type=f32)).astype(bf16)
        grad_down = grad_down + jnp.dot(activated.T, cq, preferred_element_type=f32)
        d_act = (jnp.dot(cq, w_down.T, preferred_element_type=f32) * silu_slope(pre)).astype(bf16)
        grad_up = grad_up + jnp.dot(hidden.T, d_act, preferred_element_type=f32)
        d_hidden = (cq.astype(f32) + jnp.dot(d_act, w_up.T, preferred_element_type=f32)).astype(bf16)
        d_mixed = (d_hidden.astype(f32) * gq).astype(bf16)
        d_gate = d_hidden.astype(f32) * mixed32 * gq * (1.0 - gq)
        d_mixed_mid = a2a(d_mixed.reshape(n_ctx, local_blocks, r_n, width), "ctx")
        d_mixed_mid = d_mixed_mid.reshape(all_blocks, r_n, width)
        d_first_mid = jnp.einsum("mkc,im->ikc", d_mixed_mid, w_second, preferred_element_type=f32).astype(bf16)
        grad_second = grad_second + jnp.einsum(
            "ikc,mkc->im", first_mid, d_mixed_mid, preferred_element_type=f32
        )
        d_first = a2a(d_first_mid.reshape(n_ctx, local_blocks, r_n, width), "ctx")
        d_values = d_values + jnp.einsum("dirc,jdr->ijc", d_first, wf_q, preferred_element_type=f32)
        gf_parts.append(jnp.einsum("ijc,dirc->jdr", value_blocks, d_first, preferred_element_type=f32))
        outs.append(out_q.reshape(n_ctx, local_blocks, r_n, width))
        d_hiddens.append(d_hidden.reshape(n_ctx, local_blocks, r_n, width))
        d_gates.append(d_gate.reshape(n_ctx, local_blocks, r_n, width))

    def rows_of(parts):
        return jnp.stack(parts, axis=2).transpose(1, 0, 2, 3, 4).reshape(seq_rows, width)

    output = rows_of(outs)
    d_hidden = rows_of(d_hiddens)
    d_gate = rows_of(d_gates)
    grad_first = jnp.stack(gf_parts, axis=2).reshape(block_size, block_size)
    d_projected = jnp.concatenate([d_gate, d_values.reshape(seq_rows, width)], axis=1).astype(bf16)
    grad_gate_value = jnp.dot(seq_in.T, d_projected, preferred_element_type=f32)
    grad_tokens = (
        d_hidden.astype(f32) + jnp.dot(d_projected, w_gate_value.T, preferred_element_type=f32)
    ).astype(bf16)

    grads = (grad_gate_value, grad_first, grad_second, grad_up, grad_down)
    lane = 128
    flat = jnp.concatenate([g.reshape(-1, lane) for g in grads], axis=0)
    summed = all_reduce_a2a(flat)
    scale = float(seq_rows * n_ctx * n_dp) ** (-0.5)
    summed = summed * scale
    results = []
    at = 0
    for g in grads:
        n = g.size // lane
        results.append(summed[at:at + n].reshape(g.shape))
        at += n
    return (output[None], grad_tokens[None], *results)


def solution(mesh):
    placed = (P("dp", "ctx", None), P("dp", "ctx", None), P(), P(), P(), P(), P())
    return jax.shard_map(
        body,
        mesh=mesh,
        in_specs=placed,
        out_specs=(P("dp", "ctx", None), P("dp", "ctx", None), P(), P(), P(), P(), P()),
        check_vma=False,
    )
```

```python
import jax
import jax.numpy as jnp
from jax import lax
from jax.sharding import PartitionSpec as P

CHUNKS = 1


def silu_slope(pre):
    sigma = jax.nn.sigmoid(pre)
    return sigma * (1.0 + pre * (1.0 - sigma))


def a2a(x, axis, groups=None):
    return lax.all_to_all(x, axis, 0, 0, tiled=True, axis_index_groups=groups)


def all_reduce_a2a(flat):
    n_ctx = lax.axis_size("ctx")
    n_dp = lax.axis_size("dp")
    rows, width = flat.shape
    core = lax.axis_index("ctx") % 2
    pairs = [(i, i ^ 1) for i in range(n_ctx)]
    groups = [list(range(0, n_ctx, 2)), list(range(1, n_ctx, 2))]
    chips = n_ctx // 2
    half = rows // 2
    part = half // chips
    halves = flat.reshape(2, half, width)
    mine = jnp.where(core == 0, halves[0], halves[1])
    other = jnp.where(core == 0, halves[1], halves[0])
    s1 = mine + lax.ppermute(other, "ctx", pairs)
    a = a2a(s1.reshape(chips, part, width), "ctx", groups).sum(0)
    c = a2a(jnp.broadcast_to(a[None], (n_dp, part, width)), "dp").sum(0)
    d = a2a(jnp.broadcast_to(c[None], (chips, part, width)), "ctx", groups).reshape(half, width)
    e = lax.ppermute(d, "ctx", pairs)
    return jnp.where(core == 0, jnp.concatenate([d, e]), jnp.concatenate([e, d]))


def body(tokens, cotangent, w_gate_value, w_first, w_second, w_up, w_down):
    f32 = jnp.float32
    bf16 = jnp.bfloat16
    n_ctx = lax.axis_size("ctx")
    n_dp = lax.axis_size("dp")
    seq_rows = tokens.shape[1]
    width = tokens.shape[2]
    block_size = w_first.shape[0]
    local_blocks = seq_rows // block_size
    all_blocks = w_second.shape[0]
    per_dev = block_size // n_ctx
    q_n = CHUNKS
    r_n = per_dev // q_n
    seq_in = tokens[0]
    seq_cot = cotangent[0]
    projected = jnp.dot(seq_in, w_gate_value, preferred_element_type=f32)
    gate = jax.nn.sigmoid(projected[:, :width])
    values = projected[:, width:].astype(bf16)
    value_blocks = values.reshape(local_blocks, block_size, width)
    wf = w_first.reshape(block_size, n_ctx, q_n, r_n)
    x5 = seq_in.reshape(local_blocks, n_ctx, q_n, r_n, width)
    c5 = seq_cot.reshape(local_blocks, n_ctx, q_n, r_n, width)
    g5 = gate.reshape(local_blocks, n_ctx, q_n, r_n, width)

    grad_down = jnp.zeros((w_down.shape[0], width), f32)
    grad_up = jnp.zeros((width, w_up.shape[1]), f32)
    grad_second = jnp.zeros((all_blocks, all_blocks), f32)
    d_values = jnp.zeros((local_blocks, block_size, width), f32)
    outs, d_hiddens, d_gates, gf_parts = [], [], [], []
    for q in range(q_n):
        wf_q = wf[:, :, q, :]
        first_q = jnp.einsum("ijc,jdr->dirc", value_blocks, wf_q, preferred_element_type=f32).astype(bf16)
        first_mid = a2a(first_q.reshape(n_ctx, local_blocks, r_n * width), "ctx").reshape(all_blocks, r_n * width)
        mixed_mid = jnp.dot(w_second.T, first_mid, preferred_element_type=f32).astype(bf16)
        mixed = a2a(mixed_mid.reshape(n_ctx, local_blocks, r_n * width), "ctx").reshape(n_ctx, local_blocks, r_n, width)
        mixed = mixed.reshape(-1, width)
        xq = x5[:, :, q].transpose(1, 0, 2, 3).reshape(-1, width)
        cq = c5[:, :, q].transpose(1, 0, 2, 3).reshape(-1, width)
        gq = g5[:, :, q].transpose(1, 0, 2, 3).reshape(-1, width)
        mixed32 = mixed.astype(f32)
        hidden = (xq.astype(f32) + gq * mixed32).astype(bf16)
        pre = jnp.dot(hidden, w_up, preferred_element_type=f32)
        activated = jax.nn.silu(pre).astype(bf16)
        out_q = (hidden.astype(f32) + jnp.dot(activated, w_down, preferred_element_type=f32)).astype(bf16)
        grad_down = grad_down + jnp.dot(activated.T, cq, preferred_element_type=f32)
        d_act = (jnp.dot(cq, w_down.T, preferred_element_type=f32) * silu_slope(pre)).astype(bf16)
        grad_up = grad_up + jnp.dot(hidden.T, d_act, preferred_element_type=f32)
        d_hidden = (cq.astype(f32) + jnp.dot(d_act, w_up.T, preferred_element_type=f32)).astype(bf16)
        d_mixed = (d_hidden.astype(f32) * gq).astype(bf16)
        d_gate = d_hidden.astype(f32) * mixed32 * gq * (1.0 - gq)
        d_mixed_mid = a2a(d_mixed.reshape(n_ctx, local_blocks, r_n * width), "ctx")
        d_mixed_mid = d_mixed_mid.reshape(all_blocks, r_n * width)
        d_first_mid = jnp.dot(w_second, d_mixed_mid, preferred_element_type=f32).astype(bf16)
        grad_second = grad_second + jnp.dot(first_mid, d_mixed_mid.T, preferred_element_type=f32)
        d_first = a2a(d_first_mid.reshape(n_ctx, local_blocks, r_n * width), "ctx")
        d_first = d_first.reshape(n_ctx, local_blocks, r_n, width)
        d_values = d_values + jnp.einsum("dirc,jdr->ijc", d_first, wf_q, preferred_element_type=f32)
        gf_parts.append(jnp.einsum("ijc,dirc->jdr", value_blocks, d_first, preferred_element_type=f32))
        outs.append(out_q.reshape(n_ctx, local_blocks, r_n, width))
        d_hiddens.append(d_hidden.reshape(n_ctx, local_blocks, r_n, width))
        d_gates.append(d_gate.reshape(n_ctx, local_blocks, r_n, width))

    def rows_of(parts):
        return jnp.stack(parts, axis=2).transpose(1, 0, 2, 3, 4).reshape(seq_rows, width)

    output = rows_of(outs)
    d_hidden = rows_of(d_hiddens)
    d_gate = rows_of(d_gates)
    grad_first = jnp.stack(gf_parts, axis=2).reshape(block_size, block_size)
    d_projected = jnp.concatenate([d_gate, d_values.reshape(seq_rows, width)], axis=1).astype(bf16)
    grad_gate_value = jnp.dot(seq_in.T, d_projected, preferred_element_type=f32)
    grad_tokens = (
        d_hidden.astype(f32) + jnp.dot(d_projected, w_gate_value.T, preferred_element_type=f32)
    ).astype(bf16)

    grads = (grad_gate_value, grad_first, grad_second, grad_up, grad_down)
    lane = 128
    flat = jnp.concatenate([g.reshape(-1, lane) for g in grads], axis=0)
    summed = all_reduce_a2a(flat)
    scale = float(seq_rows * n_ctx * n_dp) ** (-0.5)
    summed = summed * scale
    results = []
    at = 0
    for g in grads:
        n = g.size // lane
        results.append(summed[at:at + n].reshape(g.shape))
        at += n
    return (output[None], grad_tokens[None], *results)


def solution(mesh):
    placed = (P("dp", "ctx", None), P("dp", "ctx", None), P(), P(), P(), P(), P())
    return jax.shard_map(
        body,
        mesh=mesh,
        in_specs=placed,
        out_specs=(P("dp", "ctx", None), P("dp", "ctx", None), P(), P(), P(), P(), P()),
        check_vma=False,
    )
```

```python
import jax
import jax.numpy as jnp
from jax import lax
from jax.experimental import pallas as pl
from jax.experimental.pallas import tpu as pltpu
from jax.sharding import PartitionSpec as P

CHUNKS = 1


def silu_slope(pre):
    sigma = jax.nn.sigmoid(pre)
    return sigma * (1.0 + pre * (1.0 - sigma))


def mlp_kernel(x_ref, c_ref, g_ref, m_ref, wu_ref, wd_ref, wut_ref, wdt_ref,
               out_ref, dh_ref, dm_ref, dg_ref, gu_ref, gd_ref):
    f32 = jnp.float32
    bf16 = jnp.bfloat16
    @pl.when(pl.program_id(0) == 0)
    def _():
        gu_ref[...] = jnp.zeros_like(gu_ref)
        gd_ref[...] = jnp.zeros_like(gd_ref)
    gate = g_ref[...]
    mixed32 = m_ref[...].astype(f32)
    cot = c_ref[...]
    hidden = (x_ref[...].astype(f32) + gate * mixed32).astype(bf16)
    pre = jnp.dot(hidden, wu_ref[...], preferred_element_type=f32)
    sigma = jax.nn.sigmoid(pre)
    activated = (pre * sigma).astype(bf16)
    out_ref[...] = (hidden.astype(f32) + jnp.dot(activated, wd_ref[...], preferred_element_type=f32)).astype(bf16)
    gd_ref[...] += jnp.dot(activated.T, cot, preferred_element_type=f32)
    slope = sigma * (1.0 + pre * (1.0 - sigma))
    d_act = (jnp.dot(cot, wdt_ref[...], preferred_element_type=f32) * slope).astype(bf16)
    gu_ref[...] += jnp.dot(hidden.T, d_act, preferred_element_type=f32)
    d_hidden = (cot.astype(f32) + jnp.dot(d_act, wut_ref[...], preferred_element_type=f32)).astype(bf16)
    dh_ref[...] = d_hidden
    dh32 = d_hidden.astype(f32)
    dm_ref[...] = (dh32 * gate).astype(bf16)
    dg_ref[...] = dh32 * mixed32 * gate * (1.0 - gate)

def mlp(x, cot, gate, mixed, w_up, w_down, tile=1024):
    rows, width = x.shape
    ff = w_up.shape[1]
    f32 = jnp.float32
    bf16 = jnp.bfloat16
    row = pl.BlockSpec((tile, width), lambda i: (i, 0))
    whole = lambda shape: pl.BlockSpec(shape, lambda i: (0, 0))
    return pl.pallas_call(
        mlp_kernel,
        grid=(rows // tile,),
        in_specs=[row, row, row, row, whole((width, ff)), whole((ff, width)), whole((ff, width)), whole((width, ff))],
        out_specs=[row, row, row, row, whole((width, ff)), whole((ff, width))],
        out_shape=[jax.ShapeDtypeStruct((rows, width), bf16)] * 3 + [jax.ShapeDtypeStruct((rows, width), f32),
                   jax.ShapeDtypeStruct((width, ff), f32), jax.ShapeDtypeStruct((ff, width), f32)],
        compiler_params=pltpu.CompilerParams(dimension_semantics=("arbitrary",)),
    )(x, cot, gate, mixed, w_up, w_down, w_up.T, w_down.T)


def a2a(x, axis, groups=None):
    return lax.all_to_all(x, axis, 0, 0, tiled=True, axis_index_groups=groups)


def all_reduce_a2a(flat):
    n_ctx = lax.axis_size("ctx")
    n_dp = lax.axis_size("dp")
    rows, width = flat.shape
    core = lax.axis_index("ctx") % 2
    pairs = [(i, i ^ 1) for i in range(n_ctx)]
    groups = [list(range(0, n_ctx, 2)), list(range(1, n_ctx, 2))]
    chips = n_ctx // 2
    half = rows // 2
    part = half // chips
    piece = part // n_dp
    halves = flat.reshape(2, half, width)
    mine = jnp.where(core == 0, halves[0], halves[1])
    other = jnp.where(core == 0, halves[1], halves[0])
    s1 = mine + lax.ppermute(other, "ctx", pairs)
    a = a2a(s1.reshape(chips, part, width), "ctx", groups).sum(0)
    b = a2a(a.reshape(n_dp, piece, width), "dp").sum(0)
    c = a2a(jnp.broadcast_to(b[None], (n_dp, piece, width)), "dp").reshape(part, width)
    d = a2a(jnp.broadcast_to(c[None], (chips, part, width)), "ctx", groups).reshape(half, width)
    e = lax.ppermute(d, "ctx", pairs)
    return jnp.where(core == 0, jnp.concatenate([d, e]), jnp.concatenate([e, d]))


def body(tokens, cotangent, w_gate_value, w_first, w_second, w_up, w_down):
    f32 = jnp.float32
    bf16 = jnp.bfloat16
    n_ctx = lax.axis_size("ctx")
    n_dp = lax.axis_size("dp")
    seq_rows = tokens.shape[1]
    width = tokens.shape[2]
    block_size = w_first.shape[0]
    local_blocks = seq_rows // block_size
    all_blocks = w_second.shape[0]
    per_dev = block_size // n_ctx
    q_n = CHUNKS
    r_n = per_dev // q_n
    seq_in = tokens[0]
    seq_cot = cotangent[0]
    projected = jnp.dot(seq_in, w_gate_value, preferred_element_type=f32)
    gate = jax.nn.sigmoid(projected[:, :width])
    values = projected[:, width:].astype(bf16)
    value_blocks = values.reshape(local_blocks, block_size, width)
    wf = w_first.reshape(block_size, n_ctx, q_n, r_n)
    x5 = seq_in.reshape(local_blocks, n_ctx, q_n, r_n, width)
    c5 = seq_cot.reshape(local_blocks, n_ctx, q_n, r_n, width)
    g5 = gate.reshape(local_blocks, n_ctx, q_n, r_n, width)

    grad_down = jnp.zeros((w_down.shape[0], width), f32)
    grad_up = jnp.zeros((width, w_up.shape[1]), f32)
    grad_second = jnp.zeros((all_blocks, all_blocks), f32)
    d_values = jnp.zeros((local_blocks, block_size, width), f32)
    outs, d_hiddens, d_gates, gf_parts = [], [], [], []
    for q in range(q_n):
        wf_q = wf[:, :, q, :]
        first_q = jnp.einsum("ijc,jdr->dirc", value_blocks, wf_q, preferred_element_type=f32).astype(bf16)
        first_mid = a2a(first_q, "ctx").reshape(all_blocks, r_n, width)
        mixed_mid = jnp.einsum("ikc,im->mkc", first_mid, w_second, preferred_element_type=f32).astype(bf16)
        mixed = a2a(mixed_mid.reshape(n_ctx, local_blocks, r_n, width), "ctx")
        mixed = mixed.reshape(-1, width)
        xq = x5[:, :, q].transpose(1, 0, 2, 3).reshape(-1, width)
        cq = c5[:, :, q].transpose(1, 0, 2, 3).reshape(-1, width)
        gq = g5[:, :, q].transpose(1, 0, 2, 3).reshape(-1, width)
        out_q, d_hidden, d_mixed, d_gate, gu, gd = mlp(xq, cq, gq, mixed, w_up, w_down)
        grad_up = grad_up + gu
        grad_down = grad_down + gd
        d_mixed_mid = a2a(d_mixed.reshape(n_ctx, local_blocks, r_n, width), "ctx")
        d_mixed_mid = d_mixed_mid.reshape(all_blocks, r_n, width)
        d_first_mid = jnp.einsum("mkc,im->ikc", d_mixed_mid, w_second, preferred_element_type=f32).astype(bf16)
        grad_second = grad_second + jnp.einsum(
            "ikc,mkc->im", first_mid, d_mixed_mid, preferred_element_type=f32
        )
        d_first = a2a(d_first_mid.reshape(n_ctx, local_blocks, r_n, width), "ctx")
        d_values = d_values + jnp.einsum("dirc,jdr->ijc", d_first, wf_q, preferred_element_type=f32)
        gf_parts.append(jnp.einsum("ijc,dirc->jdr", value_blocks, d_first, preferred_element_type=f32))
        outs.append(out_q.reshape(n_ctx, local_blocks, r_n, width))
        d_hiddens.append(d_hidden.reshape(n_ctx, local_blocks, r_n, width))
        d_gates.append(d_gate.reshape(n_ctx, local_blocks, r_n, width))

    def rows_of(parts):
        return jnp.stack(parts, axis=2).transpose(1, 0, 2, 3, 4).reshape(seq_rows, width)

    output = rows_of(outs)
    d_hidden = rows_of(d_hiddens)
    d_gate = rows_of(d_gates)
    grad_first = jnp.stack(gf_parts, axis=2).reshape(block_size, block_size)
    d_projected = jnp.concatenate([d_gate, d_values.reshape(seq_rows, width)], axis=1).astype(bf16)
    grad_gate_value = jnp.dot(seq_in.T, d_projected, preferred_element_type=f32)
    grad_tokens = (
        d_hidden.astype(f32) + jnp.dot(d_projected, w_gate_value.T, preferred_element_type=f32)
    ).astype(bf16)

    grads = (grad_gate_value, grad_first, grad_second, grad_up, grad_down)
    lane = 128
    flat = jnp.concatenate([g.reshape(-1, lane) for g in grads], axis=0)
    summed = all_reduce_a2a(flat)
    scale = float(seq_rows * n_ctx * n_dp) ** (-0.5)
    summed = summed * scale
    results = []
    at = 0
    for g in grads:
        n = g.size // lane
        results.append(summed[at:at + n].reshape(g.shape))
        at += n
    return (output[None], grad_tokens[None], *results)


def solution(mesh):
    placed = (P("dp", "ctx", None), P("dp", "ctx", None), P(), P(), P(), P(), P())
    return jax.shard_map(
        body,
        mesh=mesh,
        in_specs=placed,
        out_specs=(P("dp", "ctx", None), P("dp", "ctx", None), P(), P(), P(), P(), P()),
        check_vma=False,
    )
```

```python
import jax
import jax.numpy as jnp
from jax import lax
from jax.experimental import pallas as pl
from jax.experimental.pallas import tpu as pltpu
from jax.sharding import PartitionSpec as P

CHUNKS = 1


def silu_slope(pre):
    sigma = jax.nn.sigmoid(pre)
    return sigma * (1.0 + pre * (1.0 - sigma))


def mlp_kernel(x_ref, c_ref, m_ref, wg_ref, wu_ref, wd_ref, wut_ref, wdt_ref,
               out_ref, dh_ref, dm_ref, dg_ref, gu_ref, gd_ref):
    f32 = jnp.float32
    bf16 = jnp.bfloat16
    @pl.when(pl.program_id(0) == 0)
    def _():
        gu_ref[...] = jnp.zeros_like(gu_ref)
        gd_ref[...] = jnp.zeros_like(gd_ref)
    gate = jax.nn.sigmoid(jnp.dot(x_ref[...], wg_ref[...], preferred_element_type=f32))
    mixed32 = m_ref[...].astype(f32)
    cot = c_ref[...]
    hidden = (x_ref[...].astype(f32) + gate * mixed32).astype(bf16)
    pre = jnp.dot(hidden, wu_ref[...], preferred_element_type=f32)
    sigma = jax.nn.sigmoid(pre)
    activated = (pre * sigma).astype(bf16)
    out_ref[...] = (hidden.astype(f32) + jnp.dot(activated, wd_ref[...], preferred_element_type=f32)).astype(bf16)
    gd_ref[...] += jnp.dot(activated.T, cot, preferred_element_type=f32)
    slope = sigma * (1.0 + pre * (1.0 - sigma))
    d_act = (jnp.dot(cot, wdt_ref[...], preferred_element_type=f32) * slope).astype(bf16)
    gu_ref[...] += jnp.dot(hidden.T, d_act, preferred_element_type=f32)
    d_hidden = (cot.astype(f32) + jnp.dot(d_act, wut_ref[...], preferred_element_type=f32)).astype(bf16)
    dh_ref[...] = d_hidden
    dh32 = d_hidden.astype(f32)
    dm_ref[...] = (dh32 * gate).astype(bf16)
    dg_ref[...] = (dh32 * mixed32 * gate * (1.0 - gate)).astype(bf16)

def mlp(x, cot, mixed, w_gate, w_up, w_down, tile=1024):
    rows, width = x.shape
    ff = w_up.shape[1]
    f32 = jnp.float32
    bf16 = jnp.bfloat16
    row = pl.BlockSpec((tile, width), lambda i: (i, 0))
    whole = lambda shape: pl.BlockSpec(shape, lambda i: (0, 0))
    return pl.pallas_call(
        mlp_kernel,
        grid=(rows // tile,),
        in_specs=[row, row, row, whole((width, width)), whole((width, ff)), whole((ff, width)), whole((ff, width)),
                  whole((width, ff))],
        out_specs=[row, row, row, row, whole((width, ff)), whole((ff, width))],
        out_shape=[jax.ShapeDtypeStruct((rows, width), bf16)] * 4 + [jax.ShapeDtypeStruct((width, ff), f32),
                   jax.ShapeDtypeStruct((ff, width), f32)],
        compiler_params=pltpu.CompilerParams(dimension_semantics=("arbitrary",)),
    )(x, cot, mixed, w_gate, w_up, w_down, w_up.T, w_down.T)


def a2a(x, axis, groups=None):
    return lax.all_to_all(x, axis, 0, 0, tiled=True, axis_index_groups=groups)


def all_reduce_a2a(flat):
    n_ctx = lax.axis_size("ctx")
    n_dp = lax.axis_size("dp")
    rows, width = flat.shape
    core = lax.axis_index("ctx") % 2
    pairs = [(i, i ^ 1) for i in range(n_ctx)]
    groups = [list(range(0, n_ctx, 2)), list(range(1, n_ctx, 2))]
    chips = n_ctx // 2
    half = rows // 2
    part = half // chips
    piece = part // n_dp
    halves = flat.reshape(2, half, width)
    mine = jnp.where(core == 0, halves[0], halves[1])
    other = jnp.where(core == 0, halves[1], halves[0])
    s1 = mine + lax.ppermute(other, "ctx", pairs)
    a = a2a(s1.reshape(chips, part, width), "ctx", groups).sum(0)
    b = a2a(a.reshape(n_dp, piece, width), "dp").sum(0)
    c = a2a(jnp.broadcast_to(b[None], (n_dp, piece, width)), "dp").reshape(part, width)
    d = a2a(jnp.broadcast_to(c[None], (chips, part, width)), "ctx", groups).reshape(half, width)
    e = lax.ppermute(d, "ctx", pairs)
    return jnp.where(core == 0, jnp.concatenate([d, e]), jnp.concatenate([e, d]))


def body(tokens, cotangent, w_gate_value, w_first, w_second, w_up, w_down):
    f32 = jnp.float32
    bf16 = jnp.bfloat16
    n_ctx = lax.axis_size("ctx")
    n_dp = lax.axis_size("dp")
    seq_rows = tokens.shape[1]
    width = tokens.shape[2]
    block_size = w_first.shape[0]
    local_blocks = seq_rows // block_size
    all_blocks = w_second.shape[0]
    per_dev = block_size // n_ctx
    q_n = CHUNKS
    r_n = per_dev // q_n
    seq_in = tokens[0]
    seq_cot = cotangent[0]
    values = jnp.dot(seq_in, w_gate_value[:, width:], preferred_element_type=f32).astype(bf16)
    value_blocks = values.reshape(local_blocks, block_size, width)
    wf = w_first.reshape(block_size, n_ctx, q_n, r_n)
    x5 = seq_in.reshape(local_blocks, n_ctx, q_n, r_n, width)
    c5 = seq_cot.reshape(local_blocks, n_ctx, q_n, r_n, width)

    grad_down = jnp.zeros((w_down.shape[0], width), f32)
    grad_up = jnp.zeros((width, w_up.shape[1]), f32)
    grad_second = jnp.zeros((all_blocks, all_blocks), f32)
    d_values = jnp.zeros((local_blocks, block_size, width), f32)
    outs, d_hiddens, d_gates, gf_parts = [], [], [], []
    for q in range(q_n):
        wf_q = wf[:, :, q, :]
        first_q = jnp.einsum("ijc,jdr->dirc", value_blocks, wf_q, preferred_element_type=f32).astype(bf16)
        first_mid = a2a(first_q, "ctx").reshape(all_blocks, r_n, width)
        mixed_mid = jnp.einsum("ikc,im->mkc", first_mid, w_second, preferred_element_type=f32).astype(bf16)
        mixed = a2a(mixed_mid.reshape(n_ctx, local_blocks, r_n, width), "ctx")
        mixed = mixed.reshape(-1, width)
        xq = x5[:, :, q].transpose(1, 0, 2, 3).reshape(-1, width)
        cq = c5[:, :, q].transpose(1, 0, 2, 3).reshape(-1, width)
        out_q, d_hidden, d_mixed, d_gate, gu, gd = mlp(xq, cq, mixed, w_gate_value[:, :width], w_up, w_down)
        grad_up = grad_up + gu
        grad_down = grad_down + gd
        d_mixed_mid = a2a(d_mixed.reshape(n_ctx, local_blocks, r_n, width), "ctx")
        d_mixed_mid = d_mixed_mid.reshape(all_blocks, r_n, width)
        d_first_mid = jnp.einsum("mkc,im->ikc", d_mixed_mid, w_second, preferred_element_type=f32).astype(bf16)
        grad_second = grad_second + jnp.einsum(
            "ikc,mkc->im", first_mid, d_mixed_mid, preferred_element_type=f32
        )
        d_first = a2a(d_first_mid.reshape(n_ctx, local_blocks, r_n, width), "ctx")
        d_values = d_values + jnp.einsum("dirc,jdr->ijc", d_first, wf_q, preferred_element_type=f32)
        gf_parts.append(jnp.einsum("ijc,dirc->jdr", value_blocks, d_first, preferred_element_type=f32))
        outs.append(out_q.reshape(n_ctx, local_blocks, r_n, width))
        d_hiddens.append(d_hidden.reshape(n_ctx, local_blocks, r_n, width))
        d_gates.append(d_gate.reshape(n_ctx, local_blocks, r_n, width))

    def rows_of(parts):
        return jnp.stack(parts, axis=2).transpose(1, 0, 2, 3, 4).reshape(seq_rows, width)

    output = rows_of(outs)
    d_hidden = rows_of(d_hiddens)
    d_gate = rows_of(d_gates)
    grad_first = jnp.stack(gf_parts, axis=2).reshape(block_size, block_size)
    d_projected = jnp.concatenate([d_gate, d_values.reshape(seq_rows, width)], axis=1).astype(bf16)
    grad_gate_value = jnp.dot(seq_in.T, d_projected, preferred_element_type=f32)
    grad_tokens = (
        d_hidden.astype(f32) + jnp.dot(d_projected, w_gate_value.T, preferred_element_type=f32)
    ).astype(bf16)

    grads = (grad_gate_value, grad_first, grad_second, grad_up, grad_down)
    lane = 128
    flat = jnp.concatenate([g.reshape(-1, lane) for g in grads], axis=0)
    summed = all_reduce_a2a(flat)
    scale = float(seq_rows * n_ctx * n_dp) ** (-0.5)
    summed = summed * scale
    results = []
    at = 0
    for g in grads:
        n = g.size // lane
        results.append(summed[at:at + n].reshape(g.shape))
        at += n
    return (output[None], grad_tokens[None], *results)


def solution(mesh):
    placed = (P("dp", "ctx", None), P("dp", "ctx", None), P(), P(), P(), P(), P())
    return jax.shard_map(
        body,
        mesh=mesh,
        in_specs=placed,
        out_specs=(P("dp", "ctx", None), P("dp", "ctx", None), P(), P(), P(), P(), P()),
        check_vma=False,
    )
```

```python
import jax
import jax.numpy as jnp
from jax import lax
from jax.experimental import pallas as pl
from jax.experimental.pallas import tpu as pltpu
from jax.sharding import PartitionSpec as P

CHUNKS = 1


def silu_slope(pre):
    sigma = jax.nn.sigmoid(pre)
    return sigma * (1.0 + pre * (1.0 - sigma))


def mlp_kernel(x_ref, c_ref, m_ref, wg_ref, wu_ref, wd_ref, wut_ref, wdt_ref,
               out_ref, dh_ref, dm_ref, dg_ref, gu_ref, gd_ref):
    f32 = jnp.float32
    bf16 = jnp.bfloat16
    @pl.when(pl.program_id(0) == 0)
    def _():
        gu_ref[...] = jnp.zeros_like(gu_ref)
        gd_ref[...] = jnp.zeros_like(gd_ref)
    gate = jax.nn.sigmoid(jnp.dot(x_ref[...], wg_ref[...], preferred_element_type=f32))
    mixed32 = m_ref[...].astype(f32)
    cot = c_ref[...]
    hidden = (x_ref[...].astype(f32) + gate * mixed32).astype(bf16)
    pre = jnp.dot(hidden, wu_ref[...], preferred_element_type=f32)
    sigma = jax.nn.sigmoid(pre)
    activated = (pre * sigma).astype(bf16)
    out_ref[...] = (hidden.astype(f32) + jnp.dot(activated, wd_ref[...], preferred_element_type=f32)).astype(bf16)
    gd_ref[...] += jnp.dot(activated.T, cot, preferred_element_type=f32)
    slope = sigma * (1.0 + pre * (1.0 - sigma))
    d_act = (jnp.dot(cot, wdt_ref[...], preferred_element_type=f32) * slope).astype(bf16)
    gu_ref[...] += jnp.dot(hidden.T, d_act, preferred_element_type=f32)
    d_hidden = (cot.astype(f32) + jnp.dot(d_act, wut_ref[...], preferred_element_type=f32)).astype(bf16)
    dh_ref[...] = d_hidden
    dh32 = d_hidden.astype(f32)
    dm_ref[...] = (dh32 * gate).astype(bf16)
    dg_ref[...] = (dh32 * mixed32 * gate * (1.0 - gate)).astype(bf16)

def mlp(x, cot, mixed, w_gate, w_up, w_down, tile=1024):
    rows, width = x.shape
    ff = w_up.shape[1]
    f32 = jnp.float32
    bf16 = jnp.bfloat16
    row = pl.BlockSpec((tile, width), lambda i: (i, 0))
    whole = lambda shape: pl.BlockSpec(shape, lambda i: (0, 0))
    return pl.pallas_call(
        mlp_kernel,
        grid=(rows // tile,),
        in_specs=[row, row, row, whole((width, width)), whole((width, ff)), whole((ff, width)), whole((ff, width)),
                  whole((width, ff))],
        out_specs=[row, row, row, row, whole((width, ff)), whole((ff, width))],
        out_shape=[jax.ShapeDtypeStruct((rows, width), bf16)] * 4 + [jax.ShapeDtypeStruct((width, ff), f32),
                   jax.ShapeDtypeStruct((ff, width), f32)],
        compiler_params=pltpu.CompilerParams(dimension_semantics=("arbitrary",)),
    )(x, cot, mixed, w_gate, w_up, w_down, w_up.T, w_down.T)


def mix_kernel(a_ref, f_ref, o_ref):
    a = a_ref[...]
    for kk in range(f_ref.shape[1]):
        o_ref[:, kk, :] = jnp.dot(a, f_ref[:, kk, :], preferred_element_type=jnp.float32).astype(o_ref.dtype)

def mix(a, f, kb=16):
    n, k, c = f.shape
    blk = pl.BlockSpec((n, kb, c), lambda i: (0, i, 0))
    return pl.pallas_call(
        mix_kernel,
        grid=(k // kb,),
        in_specs=[pl.BlockSpec(a.shape, lambda i: (0, 0)), blk],
        out_specs=blk,
        out_shape=jax.ShapeDtypeStruct(f.shape, jnp.bfloat16),
    )(a, f)


def a2a(x, axis, groups=None):
    return lax.all_to_all(x, axis, 0, 0, tiled=True, axis_index_groups=groups)


def all_reduce_a2a(flat):
    n_ctx = lax.axis_size("ctx")
    n_dp = lax.axis_size("dp")
    rows, width = flat.shape
    core = lax.axis_index("ctx") % 2
    pairs = [(i, i ^ 1) for i in range(n_ctx)]
    groups = [list(range(0, n_ctx, 2)), list(range(1, n_ctx, 2))]
    chips = n_ctx // 2
    half = rows // 2
    part = half // chips
    piece = part // n_dp
    halves = flat.reshape(2, half, width)
    mine = jnp.where(core == 0, halves[0], halves[1])
    other = jnp.where(core == 0, halves[1], halves[0])
    s1 = mine + lax.ppermute(other, "ctx", pairs)
    a = a2a(s1.reshape(chips, part, width), "ctx", groups).sum(0)
    b = a2a(a.reshape(n_dp, piece, width), "dp").sum(0)
    c = a2a(jnp.broadcast_to(b[None], (n_dp, piece, width)), "dp").reshape(part, width)
    d = a2a(jnp.broadcast_to(c[None], (chips, part, width)), "ctx", groups).reshape(half, width)
    e = lax.ppermute(d, "ctx", pairs)
    return jnp.where(core == 0, jnp.concatenate([d, e]), jnp.concatenate([e, d]))


def body(tokens, cotangent, w_gate_value, w_first, w_second, w_up, w_down):
    f32 = jnp.float32
    bf16 = jnp.bfloat16
    n_ctx = lax.axis_size("ctx")
    n_dp = lax.axis_size("dp")
    seq_rows = tokens.shape[1]
    width = tokens.shape[2]
    block_size = w_first.shape[0]
    local_blocks = seq_rows // block_size
    all_blocks = w_second.shape[0]
    per_dev = block_size // n_ctx
    q_n = CHUNKS
    r_n = per_dev // q_n
    seq_in = tokens[0]
    seq_cot = cotangent[0]
    values = jnp.dot(seq_in, w_gate_value[:, width:], preferred_element_type=f32).astype(bf16)
    value_blocks = values.reshape(local_blocks, block_size, width)
    wf = w_first.reshape(block_size, n_ctx, q_n, r_n)
    x5 = seq_in.reshape(local_blocks, n_ctx, q_n, r_n, width)
    c5 = seq_cot.reshape(local_blocks, n_ctx, q_n, r_n, width)

    grad_down = jnp.zeros((w_down.shape[0], width), f32)
    grad_up = jnp.zeros((width, w_up.shape[1]), f32)
    grad_second = jnp.zeros((all_blocks, all_blocks), f32)
    d_values = jnp.zeros((local_blocks, block_size, width), f32)
    outs, d_hiddens, d_gates, gf_parts = [], [], [], []
    for q in range(q_n):
        wf_q = wf[:, :, q, :]
        first_q = jnp.einsum("ijc,jdr->dirc", value_blocks, wf_q, preferred_element_type=f32).astype(bf16)
        first_mid = a2a(first_q, "ctx").reshape(all_blocks, r_n, width)
        mixed_mid = mix(w_second.T, first_mid)
        mixed = a2a(mixed_mid.reshape(n_ctx, local_blocks, r_n, width), "ctx")
        mixed = mixed.reshape(-1, width)
        xq = x5[:, :, q].transpose(1, 0, 2, 3).reshape(-1, width)
        cq = c5[:, :, q].transpose(1, 0, 2, 3).reshape(-1, width)
        out_q, d_hidden, d_mixed, d_gate, gu, gd = mlp(xq, cq, mixed, w_gate_value[:, :width], w_up, w_down)
        grad_up = grad_up + gu
        grad_down = grad_down + gd
        d_mixed_mid = a2a(d_mixed.reshape(n_ctx, local_blocks, r_n, width), "ctx")
        d_mixed_mid = d_mixed_mid.reshape(all_blocks, r_n, width)
        d_first_mid = mix(w_second, d_mixed_mid)
        grad_second = grad_second + jnp.einsum(
            "ikc,mkc->im", first_mid, d_mixed_mid, preferred_element_type=f32
        )
        d_first = a2a(d_first_mid.reshape(n_ctx, local_blocks, r_n, width), "ctx")
        d_values = d_values + jnp.einsum("dirc,jdr->ijc", d_first, wf_q, preferred_element_type=f32)
        gf_parts.append(jnp.einsum("ijc,dirc->jdr", value_blocks, d_first, preferred_element_type=f32))
        outs.append(out_q.reshape(n_ctx, local_blocks, r_n, width))
        d_hiddens.append(d_hidden.reshape(n_ctx, local_blocks, r_n, width))
        d_gates.append(d_gate.reshape(n_ctx, local_blocks, r_n, width))

    def rows_of(parts):
        return jnp.stack(parts, axis=2).transpose(1, 0, 2, 3, 4).reshape(seq_rows, width)

    output = rows_of(outs)
    d_hidden = rows_of(d_hiddens)
    d_gate = rows_of(d_gates)
    grad_first = jnp.stack(gf_parts, axis=2).reshape(block_size, block_size)
    d_projected = jnp.concatenate([d_gate, d_values.reshape(seq_rows, width)], axis=1).astype(bf16)
    grad_gate_value = jnp.dot(seq_in.T, d_projected, preferred_element_type=f32)
    grad_tokens = (
        d_hidden.astype(f32) + jnp.dot(d_projected, w_gate_value.T, preferred_element_type=f32)
    ).astype(bf16)

    grads = (grad_gate_value, grad_first, grad_second, grad_up, grad_down)
    lane = 128
    flat = jnp.concatenate([g.reshape(-1, lane) for g in grads], axis=0)
    summed = all_reduce_a2a(flat)
    scale = float(seq_rows * n_ctx * n_dp) ** (-0.5)
    summed = summed * scale
    results = []
    at = 0
    for g in grads:
        n = g.size // lane
        results.append(summed[at:at + n].reshape(g.shape))
        at += n
    return (output[None], grad_tokens[None], *results)


def solution(mesh):
    placed = (P("dp", "ctx", None), P("dp", "ctx", None), P(), P(), P(), P(), P())
    return jax.shard_map(
        body,
        mesh=mesh,
        in_specs=placed,
        out_specs=(P("dp", "ctx", None), P("dp", "ctx", None), P(), P(), P(), P(), P()),
        check_vma=False,
    )
```

```python
import jax
import jax.numpy as jnp
from jax import lax
from jax.experimental import pallas as pl
from jax.experimental.pallas import tpu as pltpu
from jax.sharding import PartitionSpec as P

CHUNKS = 1


def silu_slope(pre):
    sigma = jax.nn.sigmoid(pre)
    return sigma * (1.0 + pre * (1.0 - sigma))


def mlp_kernel(x_ref, c_ref, m_ref, wg_ref, wu_ref, wd_ref, wut_ref, wdt_ref,
               out_ref, dh_ref, dm_ref, dg_ref, gu_ref, gd_ref):
    f32 = jnp.float32
    bf16 = jnp.bfloat16
    @pl.when(pl.program_id(0) == 0)
    def _():
        gu_ref[...] = jnp.zeros_like(gu_ref)
        gd_ref[...] = jnp.zeros_like(gd_ref)
    gate = jax.nn.sigmoid(jnp.dot(x_ref[...], wg_ref[...], preferred_element_type=f32))
    mixed32 = m_ref[...].astype(f32)
    cot = c_ref[...]
    hidden = (x_ref[...].astype(f32) + gate * mixed32).astype(bf16)
    pre = jnp.dot(hidden, wu_ref[...], preferred_element_type=f32)
    sigma = jax.nn.sigmoid(pre)
    activated = (pre * sigma).astype(bf16)
    out_ref[...] = (hidden.astype(f32) + jnp.dot(activated, wd_ref[...], preferred_element_type=f32)).astype(bf16)
    gd_ref[...] += jnp.dot(activated.T, cot, preferred_element_type=f32)
    slope = sigma * (1.0 + pre * (1.0 - sigma))
    d_act = (jnp.dot(cot, wdt_ref[...], preferred_element_type=f32) * slope).astype(bf16)
    gu_ref[...] += jnp.dot(hidden.T, d_act, preferred_element_type=f32)
    d_hidden = (cot.astype(f32) + jnp.dot(d_act, wut_ref[...], preferred_element_type=f32)).astype(bf16)
    dh_ref[...] = d_hidden
    dh32 = d_hidden.astype(f32)
    dm_ref[...] = (dh32 * gate).astype(bf16)
    dg_ref[...] = (dh32 * mixed32 * gate * (1.0 - gate)).astype(bf16)

def mlp(x, cot, mixed, w_gate, w_up, w_down, tile=1024):
    rows, width = x.shape
    ff = w_up.shape[1]
    f32 = jnp.float32
    bf16 = jnp.bfloat16
    row = pl.BlockSpec((tile, width), lambda i: (i, 0))
    whole = lambda shape: pl.BlockSpec(shape, lambda i: (0, 0))
    return pl.pallas_call(
        mlp_kernel,
        grid=(rows // tile,),
        in_specs=[row, row, row, whole((width, width)), whole((width, ff)), whole((ff, width)), whole((ff, width)),
                  whole((width, ff))],
        out_specs=[row, row, row, row, whole((width, ff)), whole((ff, width))],
        out_shape=[jax.ShapeDtypeStruct((rows, width), bf16)] * 4 + [jax.ShapeDtypeStruct((width, ff), f32),
                   jax.ShapeDtypeStruct((ff, width), f32)],
        compiler_params=pltpu.CompilerParams(dimension_semantics=("arbitrary",)),
    )(x, cot, mixed, w_gate, w_up, w_down, w_up.T, w_down.T)


def a2a(x, axis, groups=None):
    return lax.all_to_all(x, axis, 0, 0, tiled=True, axis_index_groups=groups)


def all_reduce_a2a(flat):
    n_ctx = lax.axis_size("ctx")
    n_dp = lax.axis_size("dp")
    rows, width = flat.shape
    core = lax.axis_index("ctx") % 2
    pairs = [(i, i ^ 1) for i in range(n_ctx)]
    groups = [list(range(0, n_ctx, 2)), list(range(1, n_ctx, 2))]
    chips = n_ctx // 2
    half = rows // 2
    part = half // chips
    halves = flat.reshape(2, half, width)
    mine = jnp.where(core == 0, halves[0], halves[1])
    other = jnp.where(core == 0, halves[1], halves[0])
    s1 = mine + lax.ppermute(other, "ctx", pairs)
    a = a2a(s1.reshape(chips, part, width), "ctx", groups).sum(0)
    c = a
    step = 1
    while step < n_dp:
        c = c + lax.ppermute(c, "dp", [(i, i ^ step) for i in range(n_dp)])
        step *= 2
    d = a2a(jnp.broadcast_to(c[None], (chips, part, width)), "ctx", groups).reshape(half, width)
    e = lax.ppermute(d, "ctx", pairs)
    return jnp.where(core == 0, jnp.concatenate([d, e]), jnp.concatenate([e, d]))


def body(tokens, cotangent, w_gate_value, w_first, w_second, w_up, w_down):
    f32 = jnp.float32
    bf16 = jnp.bfloat16
    n_ctx = lax.axis_size("ctx")
    n_dp = lax.axis_size("dp")
    seq_rows = tokens.shape[1]
    width = tokens.shape[2]
    block_size = w_first.shape[0]
    local_blocks = seq_rows // block_size
    all_blocks = w_second.shape[0]
    per_dev = block_size // n_ctx
    q_n = CHUNKS
    r_n = per_dev // q_n
    seq_in = tokens[0]
    seq_cot = cotangent[0]
    values = jnp.dot(seq_in, w_gate_value[:, width:], preferred_element_type=f32).astype(bf16)
    value_blocks = values.reshape(local_blocks, block_size, width)
    wf = w_first.reshape(block_size, n_ctx, q_n, r_n)
    x5 = seq_in.reshape(local_blocks, n_ctx, q_n, r_n, width)
    c5 = seq_cot.reshape(local_blocks, n_ctx, q_n, r_n, width)

    grad_down = jnp.zeros((w_down.shape[0], width), f32)
    grad_up = jnp.zeros((width, w_up.shape[1]), f32)
    grad_second = jnp.zeros((all_blocks, all_blocks), f32)
    d_values = jnp.zeros((local_blocks, block_size, width), f32)
    outs, d_hiddens, d_gates, gf_parts = [], [], [], []
    for q in range(q_n):
        wf_q = wf[:, :, q, :]
        first_q = jnp.einsum("ijc,jdr->dirc", value_blocks, wf_q, preferred_element_type=f32).astype(bf16)
        first_mid = a2a(first_q, "ctx").reshape(all_blocks, r_n, width)
        mixed_mid = jnp.einsum("ikc,im->mkc", first_mid, w_second, preferred_element_type=f32).astype(bf16)
        mixed = a2a(mixed_mid.reshape(n_ctx, local_blocks, r_n, width), "ctx")
        mixed = mixed.reshape(-1, width)
        xq = x5[:, :, q].transpose(1, 0, 2, 3).reshape(-1, width)
        cq = c5[:, :, q].transpose(1, 0, 2, 3).reshape(-1, width)
        out_q, d_hidden, d_mixed, d_gate, gu, gd = mlp(xq, cq, mixed, w_gate_value[:, :width], w_up, w_down)
        grad_up = grad_up + gu
        grad_down = grad_down + gd
        d_mixed_mid = a2a(d_mixed.reshape(n_ctx, local_blocks, r_n, width), "ctx")
        d_mixed_mid = d_mixed_mid.reshape(all_blocks, r_n, width)
        d_first_mid = jnp.einsum("mkc,im->ikc", d_mixed_mid, w_second, preferred_element_type=f32).astype(bf16)
        grad_second = grad_second + jnp.einsum(
            "ikc,mkc->im", first_mid, d_mixed_mid, preferred_element_type=f32
        )
        d_first = a2a(d_first_mid.reshape(n_ctx, local_blocks, r_n, width), "ctx")
        d_values = d_values + jnp.einsum("dirc,jdr->ijc", d_first, wf_q, preferred_element_type=f32)
        gf_parts.append(jnp.einsum("ijc,dirc->jdr", value_blocks, d_first, preferred_element_type=f32))
        outs.append(out_q.reshape(n_ctx, local_blocks, r_n, width))
        d_hiddens.append(d_hidden.reshape(n_ctx, local_blocks, r_n, width))
        d_gates.append(d_gate.reshape(n_ctx, local_blocks, r_n, width))

    def rows_of(parts):
        return jnp.stack(parts, axis=2).transpose(1, 0, 2, 3, 4).reshape(seq_rows, width)

    output = rows_of(outs)
    d_hidden = rows_of(d_hiddens)
    d_gate = rows_of(d_gates)
    grad_first = jnp.stack(gf_parts, axis=2).reshape(block_size, block_size)
    d_projected = jnp.concatenate([d_gate, d_values.reshape(seq_rows, width)], axis=1).astype(bf16)
    grad_gate_value = jnp.dot(seq_in.T, d_projected, preferred_element_type=f32)
    grad_tokens = (
        d_hidden.astype(f32) + jnp.dot(d_projected, w_gate_value.T, preferred_element_type=f32)
    ).astype(bf16)

    grads = (grad_gate_value, grad_first, grad_second, grad_up, grad_down)
    lane = 128
    flat = jnp.concatenate([g.reshape(-1, lane) for g in grads], axis=0)
    summed = all_reduce_a2a(flat)
    scale = float(seq_rows * n_ctx * n_dp) ** (-0.5)
    summed = summed * scale
    results = []
    at = 0
    for g in grads:
        n = g.size // lane
        results.append(summed[at:at + n].reshape(g.shape))
        at += n
    return (output[None], grad_tokens[None], *results)


def solution(mesh):
    placed = (P("dp", "ctx", None), P("dp", "ctx", None), P(), P(), P(), P(), P())
    return jax.shard_map(
        body,
        mesh=mesh,
        in_specs=placed,
        out_specs=(P("dp", "ctx", None), P("dp", "ctx", None), P(), P(), P(), P(), P()),
        check_vma=False,
    )
```

```python
import jax
import jax.numpy as jnp
from jax import lax
from jax.experimental import pallas as pl
from jax.experimental.pallas import tpu as pltpu
from jax.sharding import PartitionSpec as P

CHUNKS = 1


def silu_slope(pre):
    sigma = jax.nn.sigmoid(pre)
    return sigma * (1.0 + pre * (1.0 - sigma))


def mlp_kernel(x_ref, c_ref, m_ref, wg_ref, wu_ref, wd_ref, wut_ref, wdt_ref,
               out_ref, dh_ref, dm_ref, dg_ref, gu_ref, gd_ref):
    f32 = jnp.float32
    bf16 = jnp.bfloat16
    @pl.when(pl.program_id(0) == 0)
    def _():
        gu_ref[...] = jnp.zeros_like(gu_ref)
        gd_ref[...] = jnp.zeros_like(gd_ref)
    gate = jax.nn.sigmoid(jnp.dot(x_ref[...], wg_ref[...], preferred_element_type=f32))
    mixed32 = m_ref[...].astype(f32)
    cot = c_ref[...]
    hidden = (x_ref[...].astype(f32) + gate * mixed32).astype(bf16)
    pre = jnp.dot(hidden, wu_ref[...], preferred_element_type=f32)
    sigma = jax.nn.sigmoid(pre)
    activated = (pre * sigma).astype(bf16)
    out_ref[...] = (hidden.astype(f32) + jnp.dot(activated, wd_ref[...], preferred_element_type=f32)).astype(bf16)
    gd_ref[...] += jnp.dot(activated.T, cot, preferred_element_type=f32)
    slope = sigma * (1.0 + pre * (1.0 - sigma))
    d_act = (jnp.dot(cot, wdt_ref[...], preferred_element_type=f32) * slope).astype(bf16)
    gu_ref[...] += jnp.dot(hidden.T, d_act, preferred_element_type=f32)
    d_hidden = (cot.astype(f32) + jnp.dot(d_act, wut_ref[...], preferred_element_type=f32)).astype(bf16)
    dh_ref[...] = d_hidden
    dh32 = d_hidden.astype(f32)
    dm_ref[...] = (dh32 * gate).astype(bf16)
    dg_ref[...] = (dh32 * mixed32 * gate * (1.0 - gate)).astype(bf16)

def mlp(x, cot, mixed, w_gate, w_up, w_down, tile=1024):
    rows, width = x.shape
    ff = w_up.shape[1]
    f32 = jnp.float32
    bf16 = jnp.bfloat16
    row = pl.BlockSpec((tile, width), lambda i: (i, 0))
    whole = lambda shape: pl.BlockSpec(shape, lambda i: (0, 0))
    return pl.pallas_call(
        mlp_kernel,
        grid=(rows // tile,),
        in_specs=[row, row, row, whole((width, width)), whole((width, ff)), whole((ff, width)), whole((ff, width)),
                  whole((width, ff))],
        out_specs=[row, row, row, row, whole((width, ff)), whole((ff, width))],
        out_shape=[jax.ShapeDtypeStruct((rows, width), bf16)] * 4 + [jax.ShapeDtypeStruct((width, ff), f32),
                   jax.ShapeDtypeStruct((ff, width), f32)],
        compiler_params=pltpu.CompilerParams(dimension_semantics=("arbitrary",)),
    )(x, cot, mixed, w_gate, w_up, w_down, w_up.T, w_down.T)


def a2a(x, axis, groups=None):
    return lax.all_to_all(x, axis, 0, 0, tiled=True, axis_index_groups=groups)


def all_reduce_a2a(flat):
    n_ctx = lax.axis_size("ctx")
    n_dp = lax.axis_size("dp")
    rows, width = flat.shape
    core = lax.axis_index("ctx") % 2
    pairs = [(i, i ^ 1) for i in range(n_ctx)]
    groups = [list(range(0, n_ctx, 2)), list(range(1, n_ctx, 2))]
    chips = n_ctx // 2
    half = rows // 2
    part = half // chips
    halves = flat.reshape(2, half, width)
    mine = jnp.where(core == 0, halves[0], halves[1])
    other = jnp.where(core == 0, halves[1], halves[0])
    s1 = mine + lax.ppermute(other, "ctx", pairs)
    chip = lax.axis_index("ctx") // 2
    a = s1
    bit_n = chips.bit_length() - 1
    for b in reversed(range(bit_n)):
        n = a.shape[0] // 2
        upper = (chip >> b) & 1
        keep = jnp.where(upper == 0, a[:n], a[n:])
        send = jnp.where(upper == 0, a[n:], a[:n])
        a = keep + lax.ppermute(send, "ctx", [(i, i ^ (2 << b)) for i in range(n_ctx)])
    c = a
    step = 1
    while step < n_dp:
        c = c + lax.ppermute(c, "dp", [(i, i ^ step) for i in range(n_dp)])
        step *= 2
    d = a2a(jnp.broadcast_to(c[None], (chips, part, width)), "ctx", groups).reshape(half, width)
    e = lax.ppermute(d, "ctx", pairs)
    return jnp.where(core == 0, jnp.concatenate([d, e]), jnp.concatenate([e, d]))


def body(tokens, cotangent, w_gate_value, w_first, w_second, w_up, w_down):
    f32 = jnp.float32
    bf16 = jnp.bfloat16
    n_ctx = lax.axis_size("ctx")
    n_dp = lax.axis_size("dp")
    seq_rows = tokens.shape[1]
    width = tokens.shape[2]
    block_size = w_first.shape[0]
    local_blocks = seq_rows // block_size
    all_blocks = w_second.shape[0]
    per_dev = block_size // n_ctx
    q_n = CHUNKS
    r_n = per_dev // q_n
    seq_in = tokens[0]
    seq_cot = cotangent[0]
    values = jnp.dot(seq_in, w_gate_value[:, width:], preferred_element_type=f32).astype(bf16)
    value_blocks = values.reshape(local_blocks, block_size, width)
    wf = w_first.reshape(block_size, n_ctx, q_n, r_n)
    x5 = seq_in.reshape(local_blocks, n_ctx, q_n, r_n, width)
    c5 = seq_cot.reshape(local_blocks, n_ctx, q_n, r_n, width)

    grad_down = jnp.zeros((w_down.shape[0], width), f32)
    grad_up = jnp.zeros((width, w_up.shape[1]), f32)
    grad_second = jnp.zeros((all_blocks, all_blocks), f32)
    d_values = jnp.zeros((local_blocks, block_size, width), f32)
    outs, d_hiddens, d_gates, gf_parts = [], [], [], []
    for q in range(q_n):
        wf_q = wf[:, :, q, :]
        first_q = jnp.einsum("ijc,jdr->dirc", value_blocks, wf_q, preferred_element_type=f32).astype(bf16)
        first_mid = a2a(first_q, "ctx").reshape(all_blocks, r_n, width)
        mixed_mid = jnp.einsum("ikc,im->mkc", first_mid, w_second, preferred_element_type=f32).astype(bf16)
        mixed = a2a(mixed_mid.reshape(n_ctx, local_blocks, r_n, width), "ctx")
        mixed = mixed.reshape(-1, width)
        xq = x5[:, :, q].transpose(1, 0, 2, 3).reshape(-1, width)
        cq = c5[:, :, q].transpose(1, 0, 2, 3).reshape(-1, width)
        out_q, d_hidden, d_mixed, d_gate, gu, gd = mlp(xq, cq, mixed, w_gate_value[:, :width], w_up, w_down)
        grad_up = grad_up + gu
        grad_down = grad_down + gd
        d_mixed_mid = a2a(d_mixed.reshape(n_ctx, local_blocks, r_n, width), "ctx")
        d_mixed_mid = d_mixed_mid.reshape(all_blocks, r_n, width)
        d_first_mid = jnp.einsum("mkc,im->ikc", d_mixed_mid, w_second, preferred_element_type=f32).astype(bf16)
        grad_second = grad_second + jnp.einsum(
            "ikc,mkc->im", first_mid, d_mixed_mid, preferred_element_type=f32
        )
        d_first = a2a(d_first_mid.reshape(n_ctx, local_blocks, r_n, width), "ctx")
        d_values = d_values + jnp.einsum("dirc,jdr->ijc", d_first, wf_q, preferred_element_type=f32)
        gf_parts.append(jnp.einsum("ijc,dirc->jdr", value_blocks, d_first, preferred_element_type=f32))
        outs.append(out_q.reshape(n_ctx, local_blocks, r_n, width))
        d_hiddens.append(d_hidden.reshape(n_ctx, local_blocks, r_n, width))
        d_gates.append(d_gate.reshape(n_ctx, local_blocks, r_n, width))

    def rows_of(parts):
        return jnp.stack(parts, axis=2).transpose(1, 0, 2, 3, 4).reshape(seq_rows, width)

    output = rows_of(outs)
    d_hidden = rows_of(d_hiddens)
    d_gate = rows_of(d_gates)
    grad_first = jnp.stack(gf_parts, axis=2).reshape(block_size, block_size)
    d_projected = jnp.concatenate([d_gate, d_values.reshape(seq_rows, width)], axis=1).astype(bf16)
    grad_gate_value = jnp.dot(seq_in.T, d_projected, preferred_element_type=f32)
    grad_tokens = (
        d_hidden.astype(f32) + jnp.dot(d_projected, w_gate_value.T, preferred_element_type=f32)
    ).astype(bf16)

    grads = (grad_gate_value, grad_first, grad_second, grad_up, grad_down)
    lane = 128
    flat = jnp.concatenate([g.reshape(-1, lane) for g in grads], axis=0)
    summed = all_reduce_a2a(flat)
    scale = float(seq_rows * n_ctx * n_dp) ** (-0.5)
    summed = summed * scale
    results = []
    at = 0
    for g in grads:
        n = g.size // lane
        results.append(summed[at:at + n].reshape(g.shape))
        at += n
    return (output[None], grad_tokens[None], *results)


def solution(mesh):
    placed = (P("dp", "ctx", None), P("dp", "ctx", None), P(), P(), P(), P(), P())
    return jax.shard_map(
        body,
        mesh=mesh,
        in_specs=placed,
        out_specs=(P("dp", "ctx", None), P("dp", "ctx", None), P(), P(), P(), P(), P()),
        check_vma=False,
    )
```

```python
import jax
import jax.numpy as jnp
from jax import lax
from jax.experimental import pallas as pl
from jax.experimental.pallas import tpu as pltpu
from jax.sharding import PartitionSpec as P

CHUNKS = 1


def silu_slope(pre):
    sigma = jax.nn.sigmoid(pre)
    return sigma * (1.0 + pre * (1.0 - sigma))


def mlp_kernel(x_ref, c_ref, m_ref, wg_ref, wu_ref, wd_ref, wut_ref, wdt_ref,
               out_ref, dh_ref, dm_ref, dg_ref, gu_ref, gd_ref):
    f32 = jnp.float32
    bf16 = jnp.bfloat16
    @pl.when(pl.program_id(0) == 0)
    def _():
        gu_ref[...] = jnp.zeros_like(gu_ref)
        gd_ref[...] = jnp.zeros_like(gd_ref)
    gate = jax.nn.sigmoid(jnp.dot(x_ref[...], wg_ref[...], preferred_element_type=f32))
    mixed32 = m_ref[...].astype(f32)
    cot = c_ref[...]
    hidden = (x_ref[...].astype(f32) + gate * mixed32).astype(bf16)
    pre = jnp.dot(hidden, wu_ref[...], preferred_element_type=f32)
    sigma = jax.nn.sigmoid(pre)
    activated = (pre * sigma).astype(bf16)
    out_ref[...] = (hidden.astype(f32) + jnp.dot(activated, wd_ref[...], preferred_element_type=f32)).astype(bf16)
    gd_ref[...] += jnp.dot(activated.T, cot, preferred_element_type=f32)
    slope = sigma * (1.0 + pre * (1.0 - sigma))
    d_act = (jnp.dot(cot, wdt_ref[...], preferred_element_type=f32) * slope).astype(bf16)
    gu_ref[...] += jnp.dot(hidden.T, d_act, preferred_element_type=f32)
    d_hidden = (cot.astype(f32) + jnp.dot(d_act, wut_ref[...], preferred_element_type=f32)).astype(bf16)
    dh_ref[...] = d_hidden
    dh32 = d_hidden.astype(f32)
    dm_ref[...] = (dh32 * gate).astype(bf16)
    dg_ref[...] = (dh32 * mixed32 * gate * (1.0 - gate)).astype(bf16)

def mlp(x, cot, mixed, w_gate, w_up, w_down, tile=2048):
    rows, width = x.shape
    ff = w_up.shape[1]
    f32 = jnp.float32
    bf16 = jnp.bfloat16
    row = pl.BlockSpec((tile, width), lambda i: (i, 0))
    whole = lambda shape: pl.BlockSpec(shape, lambda i: (0, 0))
    return pl.pallas_call(
        mlp_kernel,
        grid=(rows // tile,),
        in_specs=[row, row, row, whole((width, width)), whole((width, ff)), whole((ff, width)), whole((ff, width)),
                  whole((width, ff))],
        out_specs=[row, row, row, row, whole((width, ff)), whole((ff, width))],
        out_shape=[jax.ShapeDtypeStruct((rows, width), bf16)] * 4 + [jax.ShapeDtypeStruct((width, ff), f32),
                   jax.ShapeDtypeStruct((ff, width), f32)],
        compiler_params=pltpu.CompilerParams(dimension_semantics=("arbitrary",)),
    )(x, cot, mixed, w_gate, w_up, w_down, w_up.T, w_down.T)


def a2a(x, axis, groups=None):
    return lax.all_to_all(x, axis, 0, 0, tiled=True, axis_index_groups=groups)


def all_reduce_a2a(flat):
    n_ctx = lax.axis_size("ctx")
    n_dp = lax.axis_size("dp")
    rows, width = flat.shape
    core = lax.axis_index("ctx") % 2
    pairs = [(i, i ^ 1) for i in range(n_ctx)]
    groups = [list(range(0, n_ctx, 2)), list(range(1, n_ctx, 2))]
    chips = n_ctx // 2
    half = rows // 2
    part = half // chips
    halves = flat.reshape(2, half, width)
    mine = jnp.where(core == 0, halves[0], halves[1])
    other = jnp.where(core == 0, halves[1], halves[0])
    s1 = mine + lax.ppermute(other, "ctx", pairs)
    a = a2a(s1.reshape(chips, part, width), "ctx", groups).sum(0)
    c = a
    step = 1
    while step < n_dp:
        c = c + lax.ppermute(c, "dp", [(i, i ^ step) for i in range(n_dp)])
        step *= 2
    d = a2a(jnp.broadcast_to(c[None], (chips, part, width)), "ctx", groups).reshape(half, width)
    e = lax.ppermute(d, "ctx", pairs)
    return jnp.where(core == 0, jnp.concatenate([d, e]), jnp.concatenate([e, d]))


def body(tokens, cotangent, w_gate_value, w_first, w_second, w_up, w_down):
    f32 = jnp.float32
    bf16 = jnp.bfloat16
    n_ctx = lax.axis_size("ctx")
    n_dp = lax.axis_size("dp")
    seq_rows = tokens.shape[1]
    width = tokens.shape[2]
    block_size = w_first.shape[0]
    local_blocks = seq_rows // block_size
    all_blocks = w_second.shape[0]
    per_dev = block_size // n_ctx
    q_n = CHUNKS
    r_n = per_dev // q_n
    seq_in = tokens[0]
    seq_cot = cotangent[0]
    values = jnp.dot(seq_in, w_gate_value[:, width:], preferred_element_type=f32).astype(bf16)
    value_blocks = values.reshape(local_blocks, block_size, width)
    wf = w_first.reshape(block_size, n_ctx, q_n, r_n)
    x5 = seq_in.reshape(local_blocks, n_ctx, q_n, r_n, width)
    c5 = seq_cot.reshape(local_blocks, n_ctx, q_n, r_n, width)

    grad_down = jnp.zeros((w_down.shape[0], width), f32)
    grad_up = jnp.zeros((width, w_up.shape[1]), f32)
    grad_second = jnp.zeros((all_blocks, all_blocks), f32)
    d_values = jnp.zeros((local_blocks, block_size, width), f32)
    outs, d_hiddens, d_gates, gf_parts = [], [], [], []
    for q in range(q_n):
        wf_q = wf[:, :, q, :]
        first_q = jnp.einsum("ijc,jdr->dirc", value_blocks, wf_q, preferred_element_type=f32).astype(bf16)
        first_mid = a2a(first_q, "ctx").reshape(all_blocks, r_n, width)
        mixed_mid = jnp.einsum("ikc,im->mkc", first_mid, w_second, preferred_element_type=f32).astype(bf16)
        mixed = a2a(mixed_mid.reshape(n_ctx, local_blocks, r_n, width), "ctx")
        mixed = mixed.reshape(-1, width)
        xq = x5[:, :, q].transpose(1, 0, 2, 3).reshape(-1, width)
        cq = c5[:, :, q].transpose(1, 0, 2, 3).reshape(-1, width)
        out_q, d_hidden, d_mixed, d_gate, gu, gd = mlp(xq, cq, mixed, w_gate_value[:, :width], w_up, w_down)
        grad_up = grad_up + gu
        grad_down = grad_down + gd
        d_mixed_mid = a2a(d_mixed.reshape(n_ctx, local_blocks, r_n, width), "ctx")
        d_mixed_mid = d_mixed_mid.reshape(all_blocks, r_n, width)
        d_first_mid = jnp.einsum("mkc,im->ikc", d_mixed_mid, w_second, preferred_element_type=f32).astype(bf16)
        grad_second = grad_second + jnp.einsum(
            "ikc,mkc->im", first_mid, d_mixed_mid, preferred_element_type=f32
        )
        d_first = a2a(d_first_mid.reshape(n_ctx, local_blocks, r_n, width), "ctx")
        d_values = d_values + jnp.einsum("dirc,jdr->ijc", d_first, wf_q, preferred_element_type=f32)
        gf_parts.append(jnp.einsum("ijc,dirc->jdr", value_blocks, d_first, preferred_element_type=f32))
        outs.append(out_q.reshape(n_ctx, local_blocks, r_n, width))
        d_hiddens.append(d_hidden.reshape(n_ctx, local_blocks, r_n, width))
        d_gates.append(d_gate.reshape(n_ctx, local_blocks, r_n, width))

    def rows_of(parts):
        return jnp.stack(parts, axis=2).transpose(1, 0, 2, 3, 4).reshape(seq_rows, width)

    output = rows_of(outs)
    d_hidden = rows_of(d_hiddens)
    d_gate = rows_of(d_gates)
    grad_first = jnp.stack(gf_parts, axis=2).reshape(block_size, block_size)
    d_projected = jnp.concatenate([d_gate, d_values.reshape(seq_rows, width)], axis=1).astype(bf16)
    grad_gate_value = jnp.dot(seq_in.T, d_projected, preferred_element_type=f32)
    grad_tokens = (
        d_hidden.astype(f32) + jnp.dot(d_projected, w_gate_value.T, preferred_element_type=f32)
    ).astype(bf16)

    grads = (grad_gate_value, grad_first, grad_second, grad_up, grad_down)
    lane = 128
    flat = jnp.concatenate([g.reshape(-1, lane) for g in grads], axis=0)
    summed = all_reduce_a2a(flat)
    scale = float(seq_rows * n_ctx * n_dp) ** (-0.5)
    summed = summed * scale
    results = []
    at = 0
    for g in grads:
        n = g.size // lane
        results.append(summed[at:at + n].reshape(g.shape))
        at += n
    return (output[None], grad_tokens[None], *results)


def solution(mesh):
    placed = (P("dp", "ctx", None), P("dp", "ctx", None), P(), P(), P(), P(), P())
    return jax.shard_map(
        body,
        mesh=mesh,
        in_specs=placed,
        out_specs=(P("dp", "ctx", None), P("dp", "ctx", None), P(), P(), P(), P(), P()),
        check_vma=False,
    )
```

```python
import jax
import jax.numpy as jnp
from jax import lax
from jax.experimental import pallas as pl
from jax.experimental.pallas import tpu as pltpu
from jax.sharding import PartitionSpec as P

CHUNKS = 1


def silu_slope(pre):
    sigma = jax.nn.sigmoid(pre)
    return sigma * (1.0 + pre * (1.0 - sigma))


def mlp_kernel(x_ref, c_ref, m_ref, wg_ref, wu_ref, wd_ref, wut_ref, wdt_ref,
               out_ref, dh_ref, dm_ref, dg_ref, gu_ref, gd_ref):
    f32 = jnp.float32
    bf16 = jnp.bfloat16
    @pl.when(pl.program_id(0) == 0)
    def _():
        gu_ref[...] = jnp.zeros_like(gu_ref)
        gd_ref[...] = jnp.zeros_like(gd_ref)
    gate = jax.nn.sigmoid(jnp.dot(x_ref[...], wg_ref[...], preferred_element_type=f32))
    mixed32 = m_ref[...].astype(f32)
    cot = c_ref[...]
    hidden = (x_ref[...].astype(f32) + gate * mixed32).astype(bf16)
    pre = jnp.dot(hidden, wu_ref[...], preferred_element_type=f32)
    sigma = jax.nn.sigmoid(pre)
    activated = (pre * sigma).astype(bf16)
    out_ref[...] = (hidden.astype(f32) + jnp.dot(activated, wd_ref[...], preferred_element_type=f32)).astype(bf16)
    gd_ref[...] += jnp.dot(activated.T, cot, preferred_element_type=f32)
    slope = sigma * (1.0 + pre * (1.0 - sigma))
    d_act = (jnp.dot(cot, wdt_ref[...], preferred_element_type=f32) * slope).astype(bf16)
    gu_ref[...] += jnp.dot(hidden.T, d_act, preferred_element_type=f32)
    d_hidden = (cot.astype(f32) + jnp.dot(d_act, wut_ref[...], preferred_element_type=f32)).astype(bf16)
    dh_ref[...] = d_hidden
    dh32 = d_hidden.astype(f32)
    dm_ref[...] = (dh32 * gate).astype(bf16)
    dg_ref[...] = (dh32 * mixed32 * gate * (1.0 - gate)).astype(bf16)

def mlp(x, cot, mixed, w_gate, w_up, w_down, tile=512):
    rows, width = x.shape
    ff = w_up.shape[1]
    f32 = jnp.float32
    bf16 = jnp.bfloat16
    row = pl.BlockSpec((tile, width), lambda i: (i, 0))
    whole = lambda shape: pl.BlockSpec(shape, lambda i: (0, 0))
    return pl.pallas_call(
        mlp_kernel,
        grid=(rows // tile,),
        in_specs=[row, row, row, whole((width, width)), whole((width, ff)), whole((ff, width)), whole((ff, width)),
                  whole((width, ff))],
        out_specs=[row, row, row, row, whole((width, ff)), whole((ff, width))],
        out_shape=[jax.ShapeDtypeStruct((rows, width), bf16)] * 4 + [jax.ShapeDtypeStruct((width, ff), f32),
                   jax.ShapeDtypeStruct((ff, width), f32)],
        compiler_params=pltpu.CompilerParams(dimension_semantics=("arbitrary",)),
    )(x, cot, mixed, w_gate, w_up, w_down, w_up.T, w_down.T)


def a2a(x, axis, groups=None):
    return lax.all_to_all(x, axis, 0, 0, tiled=True, axis_index_groups=groups)


def all_reduce_a2a(flat):
    n_ctx = lax.axis_size("ctx")
    n_dp = lax.axis_size("dp")
    rows, width = flat.shape
    core = lax.axis_index("ctx") % 2
    pairs = [(i, i ^ 1) for i in range(n_ctx)]
    groups = [list(range(0, n_ctx, 2)), list(range(1, n_ctx, 2))]
    chips = n_ctx // 2
    half = rows // 2
    part = half // chips
    halves = flat.reshape(2, half, width)
    mine = jnp.where(core == 0, halves[0], halves[1])
    other = jnp.where(core == 0, halves[1], halves[0])
    s1 = mine + lax.ppermute(other, "ctx", pairs)
    a = a2a(s1.reshape(chips, part, width), "ctx", groups).sum(0)
    c = a
    step = 1
    while step < n_dp:
        c = c + lax.ppermute(c, "dp", [(i, i ^ step) for i in range(n_dp)])
        step *= 2
    d = a2a(jnp.broadcast_to(c[None], (chips, part, width)), "ctx", groups).reshape(half, width)
    e = lax.ppermute(d, "ctx", pairs)
    return jnp.where(core == 0, jnp.concatenate([d, e]), jnp.concatenate([e, d]))


def body(tokens, cotangent, w_gate_value, w_first, w_second, w_up, w_down):
    f32 = jnp.float32
    bf16 = jnp.bfloat16
    n_ctx = lax.axis_size("ctx")
    n_dp = lax.axis_size("dp")
    seq_rows = tokens.shape[1]
    width = tokens.shape[2]
    block_size = w_first.shape[0]
    local_blocks = seq_rows // block_size
    all_blocks = w_second.shape[0]
    per_dev = block_size // n_ctx
    q_n = CHUNKS
    r_n = per_dev // q_n
    seq_in = tokens[0]
    seq_cot = cotangent[0]
    values = jnp.dot(seq_in, w_gate_value[:, width:], preferred_element_type=f32).astype(bf16)
    value_blocks = values.reshape(local_blocks, block_size, width)
    wf = w_first.reshape(block_size, n_ctx, q_n, r_n)
    x5 = seq_in.reshape(local_blocks, n_ctx, q_n, r_n, width)
    c5 = seq_cot.reshape(local_blocks, n_ctx, q_n, r_n, width)

    grad_down = jnp.zeros((w_down.shape[0], width), f32)
    grad_up = jnp.zeros((width, w_up.shape[1]), f32)
    grad_second = jnp.zeros((all_blocks, all_blocks), f32)
    d_values = jnp.zeros((local_blocks, block_size, width), f32)
    outs, d_hiddens, d_gates, gf_parts = [], [], [], []
    for q in range(q_n):
        wf_q = wf[:, :, q, :]
        first_q = jnp.einsum("ijc,jdr->dirc", value_blocks, wf_q, preferred_element_type=f32).astype(bf16)
        first_mid = a2a(first_q, "ctx").reshape(all_blocks, r_n, width)
        mixed_mid = jnp.einsum("ikc,im->mkc", first_mid, w_second, preferred_element_type=f32).astype(bf16)
        mixed = a2a(mixed_mid.reshape(n_ctx, local_blocks, r_n, width), "ctx")
        mixed = mixed.reshape(-1, width)
        xq = x5[:, :, q].transpose(1, 0, 2, 3).reshape(-1, width)
        cq = c5[:, :, q].transpose(1, 0, 2, 3).reshape(-1, width)
        out_q, d_hidden, d_mixed, d_gate, gu, gd = mlp(xq, cq, mixed, w_gate_value[:, :width], w_up, w_down)
        grad_up = grad_up + gu
        grad_down = grad_down + gd
        d_mixed_mid = a2a(d_mixed.reshape(n_ctx, local_blocks, r_n, width), "ctx")
        d_mixed_mid = d_mixed_mid.reshape(all_blocks, r_n, width)
        d_first_mid = jnp.einsum("mkc,im->ikc", d_mixed_mid, w_second, preferred_element_type=f32).astype(bf16)
        grad_second = grad_second + jnp.einsum(
            "ikc,mkc->im", first_mid, d_mixed_mid, preferred_element_type=f32
        )
        d_first = a2a(d_first_mid.reshape(n_ctx, local_blocks, r_n, width), "ctx")
        d_values = d_values + jnp.einsum("dirc,jdr->ijc", d_first, wf_q, preferred_element_type=f32)
        gf_parts.append(jnp.einsum("ijc,dirc->jdr", value_blocks, d_first, preferred_element_type=f32))
        outs.append(out_q.reshape(n_ctx, local_blocks, r_n, width))
        d_hiddens.append(d_hidden.reshape(n_ctx, local_blocks, r_n, width))
        d_gates.append(d_gate.reshape(n_ctx, local_blocks, r_n, width))

    def rows_of(parts):
        return jnp.stack(parts, axis=2).transpose(1, 0, 2, 3, 4).reshape(seq_rows, width)

    output = rows_of(outs)
    d_hidden = rows_of(d_hiddens)
    d_gate = rows_of(d_gates)
    grad_first = jnp.stack(gf_parts, axis=2).reshape(block_size, block_size)
    d_projected = jnp.concatenate([d_gate, d_values.reshape(seq_rows, width)], axis=1).astype(bf16)
    grad_gate_value = jnp.dot(seq_in.T, d_projected, preferred_element_type=f32)
    grad_tokens = (
        d_hidden.astype(f32) + jnp.dot(d_projected, w_gate_value.T, preferred_element_type=f32)
    ).astype(bf16)

    grads = (grad_gate_value, grad_first, grad_second, grad_up, grad_down)
    lane = 128
    flat = jnp.concatenate([g.reshape(-1, lane) for g in grads], axis=0)
    summed = all_reduce_a2a(flat)
    scale = float(seq_rows * n_ctx * n_dp) ** (-0.5)
    summed = summed * scale
    results = []
    at = 0
    for g in grads:
        n = g.size // lane
        results.append(summed[at:at + n].reshape(g.shape))
        at += n
    return (output[None], grad_tokens[None], *results)


def solution(mesh):
    placed = (P("dp", "ctx", None), P("dp", "ctx", None), P(), P(), P(), P(), P())
    return jax.shard_map(
        body,
        mesh=mesh,
        in_specs=placed,
        out_specs=(P("dp", "ctx", None), P("dp", "ctx", None), P(), P(), P(), P(), P()),
        check_vma=False,
    )
```
